256 devices in a mesh: dp: 8 (over z), tm: 32 (over x, y, core).
Axes of the slice: x: 4, y: 4, z: 8, core: 2. Of those that a mesh axis runs over, the one named last changes fastest.
Arguments:
- clips: bfloat16 [8, 128, 16, 16, 128], P('dp', 'tm'), may hold values from -6 to 6
- segment_ids: int32 [8, 128], P('dp'), may hold values from 0 to 3, never falling along the last dimension, each value on 1 to 64 neighbouring positions
- conv_weight: bfloat16 [3456, 128], replicated, may hold values from -0.109375 to 0.109375
- cotangent: bfloat16 [8, 128, 16, 16, 128], P('dp', 'tm'), may hold values from -6 to 6
Outputs:
- activated: bfloat16 [8, 128, 16, 16, 128], P('dp', 'tm')
- grad_clips: bfloat16 [8, 128, 16, 16, 128], P('dp', 'tm')
- grad_weight: float32 [3456, 128], P('tm')
The draws below stay inside these ranges and needn't reach their ends.
Inputs may be any that keep to these rules, and one draw needn't show every extreme that they name: segment_ids never fall along a sequence; each clip has 1 to 64 frames and one has exactly that many.
All inputs are finite; a program needn't handle non-finite values.
Results may differ from the reference program's by a relative error of at most 0.013.
Values may be sent and summed in bfloat16 or wider, within the bound.
No kernel may reach another device: no remote copies, remote signals or barrier semaphores. Data moves between devices by JAX's collectives and lax.ppermute only.
A program may use at most 64 MiB of HBM per device.

```python
import math
import jax
import jax.numpy as jnp
import numpy as np
from jax import lax

C = 128
TILE_H = 16
TILE_W = 16
CLIPS = 4
GROUPS = 8
FRAMES = 128
KROWS = 3456


def steps_of(key, dims, pieces, smallest, high):
    def one(axis_at, blocks):
        draws = jax.random.uniform(jax.random.fold_in(jax.random.fold_in(key, 6), axis_at), (blocks,), jnp.float32, smallest / len(pieces), high / len(pieces))
        return jnp.repeat(jnp.exp(draws), dims[axis_at] // blocks).reshape((-1,) + (1,) * (len(dims) - axis_at - 1))

    level = one(*pieces[0])
    for cut in pieces[1:]:
        level = level * one(*cut)
    return level


def profile(count, total, most, lean):
    weights = [(1 << 20) // math.isqrt(grade ** lean) + 1 for grade in range(2, count + 1)]
    rest, given = total - most - (count - 1), [1] * (count - 1)
    while rest > 0:
        candidates = [i for i in range(count - 1) if given[i] < most]
        pool, budget = sum([weights[i] for i in candidates]), rest
        for i in candidates:
            more = min(most - given[i], max(1, budget * weights[i] // pool), rest)
            given[i] = given[i] + more
            rest = rest - more
    return np.array([most] + given)


def ragged(stream_key, count, total, bound, lean):
    if count == 2:
        one = jax.random.randint(stream_key, (), max(1, total - bound), min(bound, total - 1) + 1)
        return jnp.stack([one, total - one])
    sizes = jnp.asarray(profile(count, total, bound, lean), jnp.int32)
    pairs = (count - 1) // 2
    giver, taker = sizes[1:1 + 2 * pairs:2], sizes[2:2 + 2 * pairs:2]
    room = jnp.minimum(giver - 1, bound - taker)
    shifted = jax.random.randint(jax.random.fold_in(stream_key, 1), (pairs,), 0, 1 << 20) % (room + 1)
    sizes = sizes.at[1:1 + 2 * pairs:2].set(giver - shifted).at[2:2 + 2 * pairs:2].set(taker + shifted)
    return sizes[jax.random.permutation(jax.random.fold_in(stream_key, 2), count)]


def noise(stream_key, extent, scale, reach, pieces=(), dtype=jnp.bfloat16):
    factor_of = steps_of(stream_key, extent, pieces, -0.22, 0.18) if pieces else 1.0
    values = jax.random.normal(stream_key, extent, jnp.float32) * scale * factor_of
    return jnp.minimum(jnp.maximum(values, -reach), reach).astype(dtype)


def setup_inputs(seed: int = 0) -> dict:
    streams_of = jax.random.split(jax.random.key(seed), 5)
    return {
        "clips": noise(streams_of[0], (GROUPS, FRAMES, TILE_H, TILE_W, C), 1.0, 6.0, ((0, 8), (1, 32))),
        "segment_ids": jax.vmap(lambda own: jnp.searchsorted(jnp.cumsum(ragged(own, CLIPS, FRAMES, FRAMES // 2, 2)), jnp.arange(FRAMES), side="right"))(jax.random.split(streams_of[1], GROUPS)).reshape((GROUPS, FRAMES)).astype(jnp.int32),
        "conv_weight": noise(streams_of[2], (KROWS, C), (27 * C) ** -0.5, 0.109375),
        "cotangent": noise(streams_of[3], (GROUPS, FRAMES, TILE_H, TILE_W, C), 1.0, 6.0, ((0, 8), (1, 32))),
    }


def one_sequence(item, conv_weight):
    frames, seg, cot = item
    nfr, hh, ww, cc = frames.shape
    segp = jnp.concatenate([jnp.full((2,), -1, jnp.int32), seg.astype(jnp.int32), jnp.full((2,), -2, jnp.int32)])
    shifted_list = []
    for kt in range(3):
        d = 2 - kt
        if d > 0:
            moved = jnp.concatenate([jnp.zeros((d, hh, ww, cc), jnp.bfloat16), frames[:nfr - d]], axis=0)
        else:
            moved = frames
        keep = segp[2 - d:2 - d + nfr] == seg
        moved = jnp.where(keep[:, None, None, None], moved, jnp.zeros_like(moved))
        shifted_list.append(jnp.pad(moved, ((0, 0), (1, 1), (1, 1), (0, 0))))
    pre = jnp.zeros((nfr * hh * ww, cc), jnp.float32)
    for kt in range(3):
        for ky in range(3):
            for kx in range(3):
                base = ((kt * 3 + ky) * 3 + kx) * cc
                tap = shifted_list[kt][:, ky:ky + hh, kx:kx + ww].reshape(-1, cc)
                pre = pre + jnp.dot(tap, conv_weight[base:base + cc], preferred_element_type=jnp.float32)
    activated = jax.nn.silu(pre).astype(jnp.bfloat16)
    sig = jax.nn.sigmoid(pre)
    grad_pre = (cot.reshape(-1, cc).astype(jnp.float32) * sig * (1.0 + pre * (1.0 - sig))).astype(jnp.bfloat16)
    grads = []
    for kt in range(3):
        for ky in range(3):
            for kx in range(3):
                tap = shifted_list[kt][:, ky:ky + hh, kx:kx + ww].reshape(-1, cc)
                grads.append(lax.dot_general(tap, grad_pre, (((0,), (0,)), ((), ())), preferred_element_type=jnp.float32))
    grad_w = jnp.concatenate(grads, axis=0)
    gp = grad_pre.reshape(nfr, hh, ww, cc)
    padded = jnp.zeros((nfr, hh + 2, ww + 2, cc), jnp.float32)
    for kt in range(3):
        d = 2 - kt
        if d > 0:
            later = jnp.concatenate([gp[d:], jnp.zeros((d, hh, ww, cc), jnp.bfloat16)], axis=0)
        else:
            later = gp
        keep = segp[2 + d:2 + d + nfr] == seg
        later = jnp.where(keep[:, None, None, None], later, jnp.zeros_like(later)).reshape(-1, cc)
        for ky in range(3):
            for kx in range(3):
                base = ((kt * 3 + ky) * 3 + kx) * cc
                part = lax.dot_general(later, conv_weight[base:base + cc], (((1,), (1,)), ((), ())), preferred_element_type=jnp.float32)
                padded = padded.at[:, ky:ky + hh, kx:kx + ww].add(part.reshape(nfr, hh, ww, cc))
    grad_x = padded[:, 1:-1, 1:-1].astype(jnp.bfloat16)
    return (activated.reshape(nfr, hh, ww, cc), grad_x, grad_w)

def reference(clips, segment_ids, conv_weight, cotangent):
    activated, grad_clips, grad_each = lax.map(lambda item: one_sequence(item, conv_weight), (clips, segment_ids, cotangent))
    count = clips.shape[0] * clips.shape[1] * clips.shape[2] * clips.shape[3]
    grad_weight = lax.optimization_barrier(jnp.sum(grad_each, axis=0)) / jnp.sqrt(jnp.float32(count))
    return (activated, grad_clips, grad_weight)
```

```python
import jax
import jax.numpy as jnp
from jax import lax
from jax.sharding import PartitionSpec as P


def from_behind(value, axis, steps):
    count = lax.axis_size(axis)
    leading, last = (max(0, -steps), min(count, count - steps))
    return lax.ppermute(value, axis, [(source, source + steps) for source in range(leading, last)])


def reduce_weight_grad(grad_local):
    tm = lax.axis_size("tm")
    dp = lax.axis_size("dp")
    rows, cols = grad_local.shape
    blocks = grad_local.reshape(tm, rows // tm, cols)
    mine = lax.all_to_all(blocks, "tm", 0, 0, tiled=True).sum(axis=0)
    step = 1
    while step < dp:
        mine = mine + lax.ppermute(mine, "dp", [(i, i ^ step) for i in range(dp)])
        step *= 2
    return mine


def per_device(clips, segment_ids, conv_weight, cotangent):
    nfr = clips.shape[1]
    hh = clips.shape[2]
    ww = clips.shape[3]
    cc = clips.shape[4]
    rows = nfr * hh * ww
    earlier = from_behind(clips[:, nfr - 2 :], "tm", 1)
    extended = jnp.concatenate([earlier, clips], axis=1)[0]
    segrow = segment_ids[0]
    segp = jnp.concatenate([jnp.full((2,), -1, jnp.int32), segrow, jnp.full((2,), -2, jnp.int32)])
    start = lax.axis_index("tm") * nfr
    seglocal = lax.dynamic_slice_in_dim(segp, start, nfr + 4, 0)
    own = seglocal[2 : 2 + nfr]
    patches = []
    pre = jnp.zeros((rows, cc), jnp.float32)
    for kt in range(3):
        moved = extended[kt : kt + nfr]
        keep = seglocal[kt : kt + nfr] == own
        moved = jnp.where(keep[:, None, None, None], moved, jnp.zeros_like(moved))
        padded = jnp.pad(moved, ((0, 0), (1, 1), (1, 1), (0, 0)))
        pieces = [padded[:, ky : ky + hh, kx : kx + ww] for ky in range(3) for kx in range(3)]
        patch = jnp.concatenate(pieces, axis=3).reshape(rows, 9 * cc)
        patches.append(patch)
        pre = pre + jnp.dot(
            patch, conv_weight[kt * 9 * cc : (kt + 1) * 9 * cc], preferred_element_type=jnp.float32
        )
    activated = jax.nn.silu(pre).astype(jnp.bfloat16).reshape(clips.shape)
    sig = jax.nn.sigmoid(pre)
    grad_pre = (
        cotangent.reshape(rows, cc).astype(jnp.float32) * sig * (1.0 + pre * (1.0 - sig))
    ).astype(jnp.bfloat16)
    count = lax.axis_size("dp") * lax.axis_size("tm") * rows
    grad_local = jnp.concatenate(
        [
            lax.dot_general(
                patch, grad_pre, (((0,), (0,)), ((), ())), preferred_element_type=jnp.float32
            )
            for patch in patches
        ],
        axis=0,
    )
    grad_local = grad_local / jnp.sqrt(jnp.float32(count))
    frames_grad = grad_pre.reshape(1, nfr, hh, ww, cc)
    later_part = from_behind(frames_grad[:, :2], "tm", -1)
    grad_ext = jnp.concatenate([frames_grad, later_part], axis=1)[0]
    summed = jnp.zeros((rows, 9 * cc), jnp.float32)
    for kt in range(3):
        d = 2 - kt
        later = grad_ext[d : d + nfr]
        keep = seglocal[2 + d : 2 + d + nfr] == own
        later = jnp.where(keep[:, None, None, None], later, jnp.zeros_like(later)).reshape(rows, cc)
        summed = summed + lax.dot_general(
            later,
            conv_weight[kt * 9 * cc : (kt + 1) * 9 * cc],
            (((1,), (1,)), ((), ())),
            preferred_element_type=jnp.float32,
        )
    summed = summed.reshape(nfr, hh, ww, 9, cc)
    canvas = jnp.zeros((nfr, hh + 2, ww + 2, cc), jnp.float32)
    for ky in range(3):
        for kx in range(3):
            canvas = canvas.at[:, ky : ky + hh, kx : kx + ww].add(summed[:, :, :, ky * 3 + kx])
    grad_clips = canvas[:, 1:-1, 1:-1].astype(jnp.bfloat16).reshape(clips.shape)
    grad_weight = reduce_weight_grad(grad_local)
    return (activated, grad_clips, grad_weight)


def solution(mesh):
    return jax.shard_map(
        per_device,
        mesh=mesh,
        in_specs=(
            P("dp", "tm", None, None, None),
            P("dp", None),
            P(),
            P("dp", "tm", None, None, None),
        ),
        out_specs=(P("dp", "tm", None, None, None), P("dp", "tm", None, None, None), P("tm", None)),
        check_vma=False,
    )
```

```python
import jax
import jax.numpy as jnp
from jax import lax
from jax.sharding import PartitionSpec as P


def from_behind(value, axis, steps):
    count = lax.axis_size(axis)
    leading, last = (max(0, -steps), min(count, count - steps))
    return lax.ppermute(value, axis, [(source, source + steps) for source in range(leading, last)])


def reduce_weight_grad(grad_local):
    tm = lax.axis_size("tm")
    dp = lax.axis_size("dp")
    rows, cols = grad_local.shape
    blocks = grad_local.reshape(tm, rows // tm, cols)
    mine = lax.all_to_all(blocks, "tm", 0, 0, tiled=True).sum(axis=0)
    received = [mine] + [
        lax.ppermute(mine, "dp", [(i, (i + shift) % dp) for i in range(dp)]) for shift in range(1, dp)
    ]
    stacked = jnp.stack(received)
    me = lax.axis_index("dp")
    ordered = jnp.take(stacked, (me - jnp.arange(dp)) % dp, axis=0)
    while ordered.shape[0] > 1:
        ordered = ordered[0::2] + ordered[1::2]
    return ordered[0]


def im2col(frames, offset, hh, ww):
    padded = jnp.pad(frames, ((0, 0), (1, 1), (1, 1), (0, 0)))
    pieces = [
        padded[:, offset(ky) : offset(ky) + hh, offset(kx) : offset(kx) + ww]
        for ky in range(3)
        for kx in range(3)
    ]
    return jnp.concatenate(pieces, axis=3).reshape(-1, 9 * frames.shape[-1])


def per_device(clips, segment_ids, conv_weight, cotangent):
    nfr = clips.shape[1]
    hh = clips.shape[2]
    ww = clips.shape[3]
    cc = clips.shape[4]
    rows = nfr * hh * ww
    earlier = from_behind(clips[:, nfr - 2 :], "tm", 1)[0]
    ahead = from_behind(jnp.concatenate([clips[:, :2], cotangent[:, :2]], axis=1), "tm", -1)[0]
    frames = jnp.concatenate([earlier, clips[0], ahead[:2]], axis=0)
    cot_ext = jnp.concatenate([cotangent[0], ahead[2:]], axis=0)
    segrow = segment_ids[0]
    segp = jnp.concatenate([jnp.full((2,), -1, jnp.int32), segrow, jnp.full((2,), -2, jnp.int32)])
    start = lax.axis_index("tm") * nfr
    seglocal = lax.dynamic_slice_in_dim(segp, start, nfr + 4, 0)
    nout = nfr + 2
    centre = seglocal[2 : 2 + nout]
    pre = jnp.zeros((nout * hh * ww, cc), jnp.float32)
    patches = []
    for kt in range(3):
        moved = frames[kt : kt + nout]
        keep = seglocal[kt : kt + nout] == centre
        moved = jnp.where(keep[:, None, None, None], moved, jnp.zeros_like(moved))
        patch = im2col(moved, lambda k: k, hh, ww)
        patches.append(patch[:rows])
        pre = pre + jnp.dot(
            patch, conv_weight[kt * 9 * cc : (kt + 1) * 9 * cc], preferred_element_type=jnp.float32
        )
    sig = jax.nn.sigmoid(pre)
    activated = jax.nn.silu(pre[:rows]).astype(jnp.bfloat16).reshape(clips.shape)
    grad_pre = (
        cot_ext.reshape(nout * hh * ww, cc).astype(jnp.float32) * sig * (1.0 + pre * (1.0 - sig))
    ).astype(jnp.bfloat16)
    own_grad = grad_pre[:rows]
    count = lax.axis_size("dp") * lax.axis_size("tm") * rows
    grad_local = jnp.concatenate(
        [
            lax.dot_general(
                patch, own_grad, (((0,), (0,)), ((), ())), preferred_element_type=jnp.float32
            )
            for patch in patches
        ],
        axis=0,
    )
    grad_local = grad_local / jnp.sqrt(jnp.float32(count))
    grad_ext = grad_pre.reshape(nout, hh, ww, cc)
    own = seglocal[2 : 2 + nfr]
    summed = jnp.zeros((rows, cc), jnp.float32)
    for kt in range(3):
        d = 2 - kt
        later = grad_ext[d : d + nfr]
        keep = seglocal[2 + d : 2 + d + nfr] == own
        later = jnp.where(keep[:, None, None, None], later, jnp.zeros_like(later))
        patch = im2col(later, lambda k: 2 - k, hh, ww)
        block = conv_weight[kt * 9 * cc : (kt + 1) * 9 * cc].reshape(9, cc, cc)
        flipped = jnp.swapaxes(block, 1, 2).reshape(9 * cc, cc)
        summed = summed + jnp.dot(patch, flipped, preferred_element_type=jnp.float32)
    grad_clips = summed.astype(jnp.bfloat16).reshape(clips.shape)
    grad_weight = reduce_weight_grad(grad_local)
    return (activated, grad_clips, grad_weight)


def solution(mesh):
    return jax.shard_map(
        per_device,
        mesh=mesh,
        in_specs=(
            P("dp", "tm", None, None, None),
            P("dp", None),
            P(),
            P("dp", "tm", None, None, None),
        ),
        out_specs=(P("dp", "tm", None, None, None), P("dp", "tm", None, None, None), P("tm", None)),
        check_vma=False,
    )
```

```python
import jax
import jax.numpy as jnp
from jax import lax
from jax.sharding import Mesh, PartitionSpec as P

TM = ("chip", "core")


def from_behind(value, axis, steps):
    count = lax.axis_size(axis)
    leading, last = (max(0, -steps), min(count, count - steps))
    return lax.ppermute(value, axis, [(source, source + steps) for source in range(leading, last)])


def reduce_weight_grad(grad_local):
    chips = lax.axis_size("chip")
    cores = lax.axis_size("core")
    dp = lax.axis_size("dp")
    rows, cols = grad_local.shape
    blocks = grad_local.reshape(chips, cores, rows // (chips * cores), cols)
    core = lax.axis_index("core")
    mine = jnp.where(core == 0, blocks[:, 0], blocks[:, 1])
    other = jnp.where(core == 0, blocks[:, 1], blocks[:, 0])
    mine = mine + lax.ppermute(other, "core", [(0, 1), (1, 0)])
    mine = lax.all_to_all(mine, "chip", 0, 0, tiled=True).sum(axis=0)
    step = 1
    while step < dp:
        mine = mine + lax.ppermute(mine, "dp", [(i, i ^ step) for i in range(dp)])
        step *= 2
    return mine


def im2col(frames, offset, hh, ww):
    padded = jnp.pad(frames, ((0, 0), (1, 1), (1, 1), (0, 0)))
    pieces = [
        padded[:, offset(ky) : offset(ky) + hh, offset(kx) : offset(kx) + ww]
        for ky in range(3)
        for kx in range(3)
    ]
    return jnp.concatenate(pieces, axis=3).reshape(-1, 9 * frames.shape[-1])


def per_device(clips, segment_ids, conv_weight, cotangent):
    nfr = clips.shape[1]
    hh = clips.shape[2]
    ww = clips.shape[3]
    cc = clips.shape[4]
    rows = nfr * hh * ww
    earlier = from_behind(clips[:, nfr - 2 :], TM, 1)[0]
    ahead = from_behind(jnp.concatenate([clips[:, :2], cotangent[:, :2]], axis=1), TM, -1)[0]
    frames = jnp.concatenate([earlier, clips[0], ahead[:2]], axis=0)
    cot_ext = jnp.concatenate([cotangent[0], ahead[2:]], axis=0)
    segrow = segment_ids[0]
    segp = jnp.concatenate([jnp.full((2,), -1, jnp.int32), segrow, jnp.full((2,), -2, jnp.int32)])
    start = (lax.axis_index("chip") * lax.axis_size("core") + lax.axis_index("core")) * nfr
    seglocal = lax.dynamic_slice_in_dim(segp, start, nfr + 4, 0)
    nout = nfr + 2
    centre = seglocal[2 : 2 + nout]
    pre = jnp.zeros((nout * hh * ww, cc), jnp.float32)
    patches = []
    for kt in range(3):
        moved = frames[kt : kt + nout]
        keep = seglocal[kt : kt + nout] == centre
        moved = jnp.where(keep[:, None, None, None], moved, jnp.zeros_like(moved))
        patch = im2col(moved, lambda k: k, hh, ww)
        patches.append(patch[:rows])
        pre = pre + jnp.dot(
            patch, conv_weight[kt * 9 * cc : (kt + 1) * 9 * cc], preferred_element_type=jnp.float32
        )
    sig = jax.nn.sigmoid(pre)
    activated = jax.nn.silu(pre[:rows]).astype(jnp.bfloat16).reshape(clips.shape)
    grad_pre = (
        cot_ext.reshape(nout * hh * ww, cc).astype(jnp.float32) * sig * (1.0 + pre * (1.0 - sig))
    ).astype(jnp.bfloat16)
    own_grad = grad_pre[:rows]
    count = lax.axis_size("dp") * (lax.axis_size("chip") * lax.axis_size("core")) * rows
    grad_local = jnp.concatenate(
        [
            lax.dot_general(
                patch, own_grad, (((0,), (0,)), ((), ())), preferred_element_type=jnp.float32
            )
            for patch in patches
        ],
        axis=0,
    )
    grad_ext = grad_pre.reshape(nout, hh, ww, cc)
    own = seglocal[2 : 2 + nfr]
    summed = jnp.zeros((rows, cc), jnp.float32)
    for kt in range(3):
        d = 2 - kt
        later = grad_ext[d : d + nfr]
        keep = seglocal[2 + d : 2 + d + nfr] == own
        later = jnp.where(keep[:, None, None, None], later, jnp.zeros_like(later))
        patch = im2col(later, lambda k: 2 - k, hh, ww)
        block = conv_weight[kt * 9 * cc : (kt + 1) * 9 * cc].reshape(9, cc, cc)
        flipped = jnp.swapaxes(block, 1, 2).reshape(9 * cc, cc)
        summed = summed + jnp.dot(patch, flipped, preferred_element_type=jnp.float32)
    grad_clips = summed.astype(jnp.bfloat16).reshape(clips.shape)
    grad_weight = reduce_weight_grad(grad_local) / jnp.sqrt(jnp.float32(count))
    return (activated, grad_clips, grad_weight)


def solution(mesh):
    dp, tm = mesh.devices.shape
    cores = 2 if tm % 2 == 0 else 1
    split = Mesh(mesh.devices.reshape(dp, tm // cores, cores), ("dp", "chip", "core"))
    return jax.shard_map(
        per_device,
        mesh=split,
        in_specs=(
            P("dp", TM, None, None, None),
            P("dp", None),
            P(),
            P("dp", TM, None, None, None),
        ),
        out_specs=(P("dp", TM, None, None, None), P("dp", TM, None, None, None), P(TM, None)),
        check_vma=False,
    )
```

```python
import jax
import jax.numpy as jnp
from jax import lax
from jax.sharding import Mesh, PartitionSpec as P

TM = ("chip", "core")


def from_behind(value, axis, steps):
    count = lax.axis_size(axis)
    leading, last = (max(0, -steps), min(count, count - steps))
    return lax.ppermute(value, axis, [(source, source + steps) for source in range(leading, last)])


def reduce_weight_grad(grad_local):
    tm = lax.axis_size("chip") * lax.axis_size("core")
    dp = lax.axis_size("dp")
    rows, cols = grad_local.shape
    blocks = grad_local.reshape(tm, rows // tm, cols)
    mine = lax.all_to_all(blocks, TM, 0, 0, tiled=True).sum(axis=0)
    step = 1
    while step < dp:
        mine = mine + lax.ppermute(mine, "dp", [(i, i ^ step) for i in range(dp)])
        step *= 2
    return mine


def im2col(frames, offset, hh, ww):
    padded = jnp.pad(frames, ((0, 0), (1, 1), (1, 1), (0, 0)))
    pieces = [
        padded[:, offset(ky) : offset(ky) + hh, offset(kx) : offset(kx) + ww]
        for ky in range(3)
        for kx in range(3)
    ]
    return jnp.concatenate(pieces, axis=3).reshape(-1, 9 * frames.shape[-1])


def per_device(clips, segment_ids, conv_weight, cotangent):
    nfr = clips.shape[1]
    hh = clips.shape[2]
    ww = clips.shape[3]
    cc = clips.shape[4]
    rows = nfr * hh * ww
    earlier = from_behind(clips[:, nfr - 2 :], TM, 1)[0]
    ahead = from_behind(jnp.concatenate([clips[:, :2], cotangent[:, :2]], axis=1), TM, -1)[0]
    blank = jnp.zeros((2, hh, ww, cc), clips.dtype)
    frames = jnp.concatenate([blank, clips[0], blank], axis=0)
    cot_ext = jnp.concatenate([cotangent[0], ahead[2:]], axis=0)
    segrow = segment_ids[0]
    segp = jnp.concatenate([jnp.full((2,), -1, jnp.int32), segrow, jnp.full((2,), -2, jnp.int32)])
    start = (lax.axis_index("chip") * lax.axis_size("core") + lax.axis_index("core")) * nfr
    seglocal = lax.dynamic_slice_in_dim(segp, start, nfr + 4, 0)
    nout = nfr + 2
    frame_rows = hh * ww
    centre = seglocal[2 : 2 + nout]
    pre = jnp.zeros((nout * frame_rows, cc), jnp.float32)
    patches = []
    for kt in range(3):
        moved = frames[kt : kt + nout]
        keep = seglocal[kt : kt + nout] == centre
        moved = jnp.where(keep[:, None, None, None], moved, jnp.zeros_like(moved))
        patch = im2col(moved, lambda k: k, hh, ww)
        patches.append(patch[:rows])
        pre = pre + jnp.dot(
            patch, conv_weight[kt * 9 * cc : (kt + 1) * 9 * cc], preferred_element_type=jnp.float32
        )
    halo = jnp.concatenate([earlier, ahead[:2]], axis=0)
    halo_patch = im2col(halo, lambda k: k, hh, ww).reshape(4, frame_rows, 9 * cc)
    terms = ((0, 0, 0), (0, 1, 1), (1, 1, 0), (nfr, 2, 2), (nfr + 1, 2, 1), (nfr + 1, 3, 2))
    fixes = [jnp.zeros((frame_rows, cc), jnp.float32) for _ in range(nout)]
    for t, h, kt in terms:
        keep = (seglocal[t + kt] == seglocal[t + 2]).astype(jnp.float32)
        part = jnp.dot(
            halo_patch[h], conv_weight[kt * 9 * cc : (kt + 1) * 9 * cc], preferred_element_type=jnp.float32
        )
        fixes[t] = fixes[t] + keep * part
    pre = pre + jnp.concatenate(fixes, axis=0)
    sig = jax.nn.sigmoid(pre)
    activated = jax.nn.silu(pre[:rows]).astype(jnp.bfloat16).reshape(clips.shape)
    grad_pre = (
        cot_ext.reshape(nout * hh * ww, cc).astype(jnp.float32) * sig * (1.0 + pre * (1.0 - sig))
    ).astype(jnp.bfloat16)
    own_grad = grad_pre[:rows]
    count = lax.axis_size("dp") * (lax.axis_size("chip") * lax.axis_size("core")) * rows
    per_tap = [
        lax.dot_general(patch, own_grad, (((0,), (0,)), ((), ())), preferred_element_type=jnp.float32)
        for patch in patches
    ]
    for t, h, kt in terms:
        if t < nfr:
            keep = (seglocal[t + kt] == seglocal[t + 2]).astype(jnp.float32)
            per_tap[kt] = per_tap[kt] + keep * lax.dot_general(
                halo_patch[h],
                own_grad[t * frame_rows : (t + 1) * frame_rows],
                (((0,), (0,)), ((), ())),
                preferred_element_type=jnp.float32,
            )
    grad_local = jnp.concatenate(per_tap, axis=0)
    grad_ext = grad_pre.reshape(nout, hh, ww, cc)
    own = seglocal[2 : 2 + nfr]
    summed = jnp.zeros((rows, cc), jnp.float32)
    for kt in range(3):
        d = 2 - kt
        later = grad_ext[d : d + nfr]
        keep = seglocal[2 + d : 2 + d + nfr] == own
        later = jnp.where(keep[:, None, None, None], later, jnp.zeros_like(later))
        patch = im2col(later, lambda k: 2 - k, hh, ww)
        block = conv_weight[kt * 9 * cc : (kt + 1) * 9 * cc].reshape(9, cc, cc)
        flipped = jnp.swapaxes(block, 1, 2).reshape(9 * cc, cc)
        summed = summed + jnp.dot(patch, flipped, preferred_element_type=jnp.float32)
    grad_clips = summed.astype(jnp.bfloat16).reshape(clips.shape)
    grad_weight = reduce_weight_grad(grad_local) / jnp.sqrt(jnp.float32(count))
    return (activated, grad_clips, grad_weight)


def solution(mesh):
    dp, tm = mesh.devices.shape
    cores = 2 if tm % 2 == 0 else 1
    split = Mesh(mesh.devices.reshape(dp, tm // cores, cores), ("dp", "chip", "core"))
    return jax.shard_map(
        per_device,
        mesh=split,
        in_specs=(
            P("dp", TM, None, None, None),
            P("dp", None),
            P(),
            P("dp", TM, None, None, None),
        ),
        out_specs=(P("dp", TM, None, None, None), P("dp", TM, None, None, None), P(TM, None)),
        check_vma=False,
    )
```

```python
import jax
import jax.numpy as jnp
from jax import lax
from jax.sharding import Mesh, PartitionSpec as P

TM = ("chip", "core")


def from_behind(value, axis, steps):
    count = lax.axis_size(axis)
    leading, last = (max(0, -steps), min(count, count - steps))
    return lax.ppermute(value, axis, [(source, source + steps) for source in range(leading, last)])


def reduce_weight_grad(grad_local):
    tm = lax.axis_size("chip") * lax.axis_size("core")
    dp = lax.axis_size("dp")
    rows, cols = grad_local.shape
    blocks = grad_local.reshape(tm, rows // tm, cols)
    mine = lax.all_to_all(blocks, TM, 0, 0, tiled=True).sum(axis=0)
    step = 1
    while step < dp:
        mine = mine + lax.ppermute(mine, "dp", [(i, i ^ step) for i in range(dp)])
        step *= 2
    return mine


def im2col(frames, offset, hh, ww):
    padded = jnp.pad(frames, ((0, 0), (1, 1), (1, 1), (0, 0)))
    pieces = [
        padded[:, offset(ky) : offset(ky) + hh, offset(kx) : offset(kx) + ww]
        for ky in range(3)
        for kx in range(3)
    ]
    return jnp.concatenate(pieces, axis=3).reshape(-1, 9 * frames.shape[-1])


def per_device(clips, segment_ids, conv_weight, cotangent):
    nfr = clips.shape[1]
    hh = clips.shape[2]
    ww = clips.shape[3]
    cc = clips.shape[4]
    rows = nfr * hh * ww
    earlier = from_behind(clips[:, nfr - 2 :], TM, 1)[0]
    ahead = from_behind(jnp.concatenate([clips[:, :2], cotangent[:, :2]], axis=1), TM, -1)[0]
    frames = jnp.concatenate([earlier, clips[0], ahead[:2]], axis=0)
    cot_ext = jnp.concatenate([cotangent[0], ahead[2:]], axis=0)
    segrow = segment_ids[0]
    segp = jnp.concatenate([jnp.full((2,), -1, jnp.int32), segrow, jnp.full((2,), -2, jnp.int32)])
    start = (lax.axis_index("chip") * lax.axis_size("core") + lax.axis_index("core")) * nfr
    seglocal = lax.dynamic_slice_in_dim(segp, start, nfr + 4, 0)
    nout = nfr + 2
    centre = seglocal[2 : 2 + nout]
    pre = jnp.zeros((nout * hh * ww, cc), jnp.float32)
    patches = []
    for kt in range(3):
        moved = frames[kt : kt + nout]
        keep = seglocal[kt : kt + nout] == centre
        moved = jnp.where(keep[:, None, None, None], moved, jnp.zeros_like(moved))
        patch = im2col(moved, lambda k: k, hh, ww)
        patches.append(patch[:rows])
        pre = pre + jnp.dot(
            patch, conv_weight[kt * 9 * cc : (kt + 1) * 9 * cc], preferred_element_type=jnp.float32
        )
    sig = jax.nn.sigmoid(pre)
    activated = jax.nn.silu(pre[:rows]).astype(jnp.bfloat16).reshape(clips.shape)
    grad_pre = (
        cot_ext.reshape(nout * hh * ww, cc).astype(jnp.float32) * sig * (1.0 + pre * (1.0 - sig))
    ).astype(jnp.bfloat16)
    own_grad = grad_pre[:rows]
    count = lax.axis_size("dp") * (lax.axis_size("chip") * lax.axis_size("core")) * rows
    grad_local = jnp.concatenate(
        [
            lax.dot_general(
                patch, own_grad, (((0,), (0,)), ((), ())), preferred_element_type=jnp.float32
            )
            for patch in patches
        ],
        axis=0,
    )
    grad_ext = grad_pre.reshape(nout, hh, ww, cc)
    own = seglocal[2 : 2 + nfr]
    summed = jnp.zeros((rows, cc), jnp.float32)
    for kt in range(3):
        d = 2 - kt
        later = grad_ext[d : d + nfr]
        keep = seglocal[2 + d : 2 + d + nfr] == own
        later = jnp.where(keep[:, None, None, None], later, jnp.zeros_like(later))
        patch = im2col(later, lambda k: 2 - k, hh, ww)
        block = conv_weight[kt * 9 * cc : (kt + 1) * 9 * cc].reshape(9, cc, cc)
        flipped = jnp.swapaxes(block, 1, 2).reshape(9 * cc, cc)
        summed = summed + jnp.dot(patch, flipped, preferred_element_type=jnp.float32)
    grad_clips = summed.astype(jnp.bfloat16).reshape(clips.shape)
    grad_weight = reduce_weight_grad(grad_local) / jnp.sqrt(jnp.float32(count))
    return (activated, grad_clips, grad_weight)


def solution(mesh):
    dp, tm = mesh.devices.shape
    cores = 2 if tm % 2 == 0 else 1
    split = Mesh(mesh.devices.reshape(dp, tm // cores, cores), ("dp", "chip", "core"))
    return jax.shard_map(
        per_device,
        mesh=split,
        in_specs=(
            P("dp", TM, None, None, None),
            P("dp", None),
            P(),
            P("dp", TM, None, None, None),
        ),
        out_specs=(P("dp", TM, None, None, None), P("dp", TM, None, None, None), P(TM, None)),
        check_vma=False,
    )
```

```python
import functools

import jax
import jax.numpy as jnp
from jax import lax
from jax.experimental import pallas as pl
from jax.experimental.pallas import tpu as pltpu
from jax.sharding import Mesh, PartitionSpec as P

TM = ("chip", "core")


def from_behind(value, axis, steps):
    count = lax.axis_size(axis)
    leading, last = (max(0, -steps), min(count, count - steps))
    return lax.ppermute(value, axis, [(source, source + steps) for source in range(leading, last)])


def reduce_weight_grad(grad_local):
    tm = lax.axis_size("chip") * lax.axis_size("core")
    dp = lax.axis_size("dp")
    rows, cols = grad_local.shape
    blocks = grad_local.reshape(tm, rows // tm, cols)
    mine = lax.all_to_all(blocks, TM, 0, 0, tiled=True).sum(axis=0)
    step = 1
    while step < dp:
        mine = mine + lax.ppermute(mine, "dp", [(i, i ^ step) for i in range(dp)])
        step *= 2
    return mine


def im2col(frames, offset, hh, ww):
    padded = jnp.pad(frames, ((0, 0), (1, 1), (1, 1), (0, 0)))
    pieces = [
        padded[:, offset(ky) : offset(ky) + hh, offset(kx) : offset(kx) + ww]
        for ky in range(3)
        for kx in range(3)
    ]
    return jnp.concatenate(pieces, axis=3).reshape(-1, 9 * frames.shape[-1])


def forward_kernel(hh, ww, nout, nfr, mask_ref, xe_ref, ce_ref, w_ref, act_ref, gp_ref, gw_ref, col_ref, pad_ref, acc_ref):
    frame = hh * ww
    cc = xe_ref.shape[1]
    taps = 9 * cc
    lead = 2 * ww
    r = lax.broadcasted_iota(jnp.int32, (frame, cc), 0)
    i = r // ww
    j = r % ww
    pad_ref[...] = jnp.zeros_like(pad_ref)
    for f in range(nout + 2):
        pad_ref[pl.ds(lead, frame), :] = xe_ref[pl.ds(f * frame, frame), :].astype(jnp.float32)
        for ky in range(3):
            for kx in range(3):
                dy, dx = ky - 1, kx - 1
                s = pad_ref[pl.ds(lead + dy * ww + dx, frame), :]
                valid = (i + dy >= 0) & (i + dy < hh) & (j + dx >= 0) & (j + dx < ww)
                s = jnp.where(valid, s, 0.0)
                col_ref[f, :, pl.ds((ky * 3 + kx) * cc, cc)] = s.astype(col_ref.dtype)
    for t in range(nout):
        pre = jnp.zeros((frame, cc), jnp.float32)
        for kt in range(3):
            part = jnp.dot(col_ref[t + kt], w_ref[pl.ds(kt * taps, taps), :], preferred_element_type=jnp.float32)
            pre = pre + mask_ref[kt, t] * part
        sig = 1.0 / (1.0 + jnp.exp(-pre))
        if t < nfr:
            act_ref[pl.ds(t * frame, frame), :] = (pre * sig).astype(act_ref.dtype)
        cot = ce_ref[pl.ds(t * frame, frame), :].astype(jnp.float32)
        gp_ref[pl.ds(t * frame, frame), :] = (cot * sig * (1.0 + pre * (1.0 - sig))).astype(gp_ref.dtype)
    acc_ref[...] = jnp.zeros_like(acc_ref)
    for t in range(nfr):
        g = gp_ref[pl.ds(t * frame, frame), :].astype(jnp.float32)
        gt = jnp.transpose(g).astype(col_ref.dtype)
        for kt in range(3):
            part = jnp.dot(gt, col_ref[t + kt], preferred_element_type=jnp.float32)
            acc_ref[kt] = acc_ref[kt] + mask_ref[kt, t] * part
    for kt in range(3):
        gw_ref[pl.ds(kt * taps, taps), :] = jnp.transpose(acc_ref[kt])


def forward_call(mask, xe, ce, w, hh, ww, nout, nfr):
    frame = hh * ww
    cc = xe.shape[1]
    krows = w.shape[0]
    vmem = pl.BlockSpec(memory_space=pltpu.VMEM)
    flops = 2 * 3 * frame * 9 * cc * cc * (nout + nfr)
    return pl.pallas_call(
        functools.partial(forward_kernel, hh, ww, nout, nfr),
        out_shape=(
            jax.ShapeDtypeStruct((nfr * frame, cc), jnp.bfloat16),
            jax.ShapeDtypeStruct((nout * frame, cc), jnp.bfloat16),
            jax.ShapeDtypeStruct((krows, cc), jnp.float32),
        ),
        in_specs=[pl.BlockSpec(memory_space=pltpu.SMEM), vmem, vmem, vmem],
        out_specs=(vmem, vmem, vmem),
        scratch_shapes=[
            pltpu.VMEM((nout + 2, frame, 9 * cc), jnp.bfloat16),
            pltpu.VMEM((frame + 4 * ww, cc), jnp.float32),
            pltpu.VMEM((3, cc, 9 * cc), jnp.float32),
        ],
        compiler_params=pltpu.CompilerParams(vmem_limit_bytes=48 * 1024 * 1024),
        cost_estimate=pl.CostEstimate(
            flops=flops, transcendentals=nout * frame * cc, bytes_accessed=2 * (xe.size + ce.size + w.size) + 4 * krows * cc
        ),
    )(mask, xe, ce, w)


def per_device(clips, segment_ids, conv_weight, cotangent):
    nfr = clips.shape[1]
    hh = clips.shape[2]
    ww = clips.shape[3]
    cc = clips.shape[4]
    rows = nfr * hh * ww
    earlier = from_behind(clips[:, nfr - 2 :], TM, 1)[0]
    ahead = from_behind(jnp.concatenate([clips[:, :2], cotangent[:, :2]], axis=1), TM, -1)[0]
    frames = jnp.concatenate([earlier, clips[0], ahead[:2]], axis=0)
    cot_ext = jnp.concatenate([cotangent[0], ahead[2:]], axis=0)
    segrow = segment_ids[0]
    segp = jnp.concatenate([jnp.full((2,), -1, jnp.int32), segrow, jnp.full((2,), -2, jnp.int32)])
    start = (lax.axis_index("chip") * lax.axis_size("core") + lax.axis_index("core")) * nfr
    seglocal = lax.dynamic_slice_in_dim(segp, start, nfr + 4, 0)
    nout = nfr + 2
    centre = seglocal[2 : 2 + nout]
    mask = jnp.stack([(seglocal[kt : kt + nout] == centre) for kt in range(3)]).astype(jnp.float32)
    act, grad_pre, grad_local = forward_call(
        mask, frames.reshape(-1, cc), cot_ext.reshape(-1, cc), conv_weight, hh, ww, nout, nfr
    )
    activated = act.reshape(clips.shape)
    count = lax.axis_size("dp") * (lax.axis_size("chip") * lax.axis_size("core")) * rows
    grad_ext = grad_pre.reshape(nout, hh, ww, cc)
    own = seglocal[2 : 2 + nfr]
    summed = jnp.zeros((rows, cc), jnp.float32)
    for kt in range(3):
        d = 2 - kt
        later = grad_ext[d : d + nfr]
        keep = seglocal[2 + d : 2 + d + nfr] == own
        later = jnp.where(keep[:, None, None, None], later, jnp.zeros_like(later))
        patch = im2col(later, lambda k: 2 - k, hh, ww)
        block = conv_weight[kt * 9 * cc : (kt + 1) * 9 * cc].reshape(9, cc, cc)
        flipped = jnp.swapaxes(block, 1, 2).reshape(9 * cc, cc)
        summed = summed + jnp.dot(patch, flipped, preferred_element_type=jnp.float32)
    grad_clips = summed.astype(jnp.bfloat16).reshape(clips.shape)
    grad_weight = reduce_weight_grad(grad_local) / jnp.sqrt(jnp.float32(count))
    return (activated, grad_clips, grad_weight)


def solution(mesh):
    dp, tm = mesh.devices.shape
    cores = 2 if tm % 2 == 0 else 1
    split = Mesh(mesh.devices.reshape(dp, tm // cores, cores), ("dp", "chip", "core"))
    return jax.shard_map(
        per_device,
        mesh=split,
        in_specs=(
            P("dp", TM, None, None, None),
            P("dp", None),
            P(),
            P("dp", TM, None, None, None),
        ),
        out_specs=(P("dp", TM, None, None, None), P("dp", TM, None, None, None), P(TM, None)),
        check_vma=False,
    )
```

```python
import functools

import jax
import jax.numpy as jnp
from jax import lax
from jax.experimental import pallas as pl
from jax.experimental.pallas import tpu as pltpu
from jax.sharding import Mesh, PartitionSpec as P

TM = ("chip", "core")


def from_behind(value, axis, steps):
    count = lax.axis_size(axis)
    leading, last = (max(0, -steps), min(count, count - steps))
    return lax.ppermute(value, axis, [(source, source + steps) for source in range(leading, last)])


def reduce_weight_grad(grad_local):
    tm = lax.axis_size("chip") * lax.axis_size("core")
    dp = lax.axis_size("dp")
    mine = lax.all_to_all(grad_local, TM, 0, 0, tiled=True).sum(axis=0)
    step = 1
    while step < dp:
        mine = mine + lax.ppermute(mine, "dp", [(i, i ^ step) for i in range(dp)])
        step *= 2
    return mine


def im2col(frames, offset, hh, ww):
    padded = jnp.pad(frames, ((0, 0), (1, 1), (1, 1), (0, 0)))
    pieces = [
        padded[:, offset(ky) : offset(ky) + hh, offset(kx) : offset(kx) + ww]
        for ky in range(3)
        for kx in range(3)
    ]
    return jnp.concatenate(pieces, axis=3).reshape(-1, 9 * frames.shape[-1])


def forward_kernel(hh, ww, nout, nfr, mask_ref, early_ref, own_ref, ahead_ref, cot_ref, w_ref, act_ref, gp_ref, gw_ref, col_ref, pad_ref, acc_ref, flat_ref):
    frame = hh * ww
    cc = own_ref.shape[1]
    taps = 9 * cc
    lead = 2 * ww
    r = lax.broadcasted_iota(jnp.int32, (frame, cc), 0)
    i = r // ww
    j = r % ww
    pad_ref[...] = jnp.zeros_like(pad_ref)
    for f in range(nout + 2):
        if f < 2:
            source = early_ref[pl.ds(f * frame, frame), :]
        elif f < nfr + 2:
            source = own_ref[pl.ds((f - 2) * frame, frame), :]
        else:
            source = ahead_ref[pl.ds((f - nfr - 2) * frame, frame), :]
        pad_ref[pl.ds(lead, frame), :] = source.astype(jnp.float32)
        for ky in range(3):
            for kx in range(3):
                dy, dx = ky - 1, kx - 1
                s = pad_ref[pl.ds(lead + dy * ww + dx, frame), :]
                valid = (i + dy >= 0) & (i + dy < hh) & (j + dx >= 0) & (j + dx < ww)
                s = jnp.where(valid, s, 0.0)
                col_ref[f, :, pl.ds((ky * 3 + kx) * cc, cc)] = s.astype(col_ref.dtype)
    for t in range(nout):
        pre = jnp.zeros((frame, cc), jnp.float32)
        for kt in range(3):
            part = jnp.dot(col_ref[t + kt], w_ref[pl.ds(kt * taps, taps), :], preferred_element_type=jnp.float32)
            pre = pre + mask_ref[kt, t] * part
        sig = 1.0 / (1.0 + jnp.exp(-pre))
        if t < nfr:
            act_ref[pl.ds(t * frame, frame), :] = (pre * sig).astype(act_ref.dtype)
        if t < nfr:
            cot = cot_ref[pl.ds(t * frame, frame), :].astype(jnp.float32)
        else:
            cot = ahead_ref[pl.ds((t - nfr + 2) * frame, frame), :].astype(jnp.float32)
        gp_ref[pl.ds(t * frame, frame), :] = (cot * sig * (1.0 + pre * (1.0 - sig))).astype(gp_ref.dtype)
    acc_ref[...] = jnp.zeros_like(acc_ref)
    for t in range(nfr):
        g = gp_ref[pl.ds(t * frame, frame), :].astype(jnp.float32)
        gt = jnp.transpose(g).astype(col_ref.dtype)
        for kt in range(3):
            part = jnp.dot(gt, col_ref[t + kt], preferred_element_type=jnp.float32)
            acc_ref[kt] = acc_ref[kt] + mask_ref[kt, t] * part
    for kt in range(3):
        flat_ref[pl.ds(kt * taps, taps), :] = jnp.transpose(acc_ref[kt])
    blocks, share = gw_ref.shape[0], gw_ref.shape[1]
    for b in range(blocks):
        gw_ref[b] = flat_ref[pl.ds(b * share, share), :]


def forward_call(mask, early, own, ahead, cot, w, hh, ww, nout, nfr, blocks):
    frame = hh * ww
    cc = own.shape[1]
    krows = w.shape[0]
    vmem = pl.BlockSpec(memory_space=pltpu.VMEM)
    flops = 2 * 3 * frame * 9 * cc * cc * (nout + nfr)
    return pl.pallas_call(
        functools.partial(forward_kernel, hh, ww, nout, nfr),
        out_shape=(
            jax.ShapeDtypeStruct((nfr * frame, cc), jnp.bfloat16),
            jax.ShapeDtypeStruct((nout * frame, cc), jnp.bfloat16),
            jax.ShapeDtypeStruct((blocks, krows // blocks, cc), jnp.float32),
        ),
        in_specs=[pl.BlockSpec(memory_space=pltpu.SMEM), vmem, vmem, vmem, vmem, vmem],
        out_specs=(vmem, vmem, vmem),
        scratch_shapes=[
            pltpu.VMEM((nout + 2, frame, 9 * cc), jnp.bfloat16),
            pltpu.VMEM((frame + 4 * ww, cc), jnp.float32),
            pltpu.VMEM((3, cc, 9 * cc), jnp.float32),
            pltpu.VMEM((krows, cc), jnp.float32),
        ],
        compiler_params=pltpu.CompilerParams(vmem_limit_bytes=48 * 1024 * 1024),
        cost_estimate=pl.CostEstimate(
            flops=flops,
            transcendentals=nout * frame * cc,
            bytes_accessed=2 * (early.size + own.size + ahead.size + cot.size + w.size) + 4 * krows * cc,
        ),
    )(mask, early, own, ahead, cot, w)


def per_device(clips, segment_ids, conv_weight, cotangent):
    nfr = clips.shape[1]
    hh = clips.shape[2]
    ww = clips.shape[3]
    cc = clips.shape[4]
    rows = nfr * hh * ww
    earlier = from_behind(clips[:, nfr - 2 :], TM, 1)[0]
    ahead = from_behind(jnp.concatenate([clips[:, :2], cotangent[:, :2]], axis=1), TM, -1)[0]
    segrow = segment_ids[0]
    segp = jnp.concatenate([jnp.full((2,), -1, jnp.int32), segrow, jnp.full((2,), -2, jnp.int32)])
    start = (lax.axis_index("chip") * lax.axis_size("core") + lax.axis_index("core")) * nfr
    seglocal = lax.dynamic_slice_in_dim(segp, start, nfr + 4, 0)
    nout = nfr + 2
    centre = seglocal[2 : 2 + nout]
    mask = jnp.stack([(seglocal[kt : kt + nout] == centre) for kt in range(3)]).astype(jnp.float32)
    tm = lax.axis_size("chip") * lax.axis_size("core")
    act, grad_pre, grad_local = forward_call(
        mask,
        earlier.reshape(-1, cc),
        clips.reshape(-1, cc),
        ahead.reshape(-1, cc),
        cotangent.reshape(-1, cc),
        conv_weight,
        hh,
        ww,
        nout,
        nfr,
        tm,
    )
    activated = act.reshape(clips.shape)
    count = lax.axis_size("dp") * (lax.axis_size("chip") * lax.axis_size("core")) * rows
    grad_ext = grad_pre.reshape(nout, hh, ww, cc)
    own = seglocal[2 : 2 + nfr]
    summed = jnp.zeros((rows, cc), jnp.float32)
    for kt in range(3):
        d = 2 - kt
        later = grad_ext[d : d + nfr]
        keep = seglocal[2 + d : 2 + d + nfr] == own
        later = jnp.where(keep[:, None, None, None], later, jnp.zeros_like(later))
        patch = im2col(later, lambda k: 2 - k, hh, ww)
        block = conv_weight[kt * 9 * cc : (kt + 1) * 9 * cc].reshape(9, cc, cc)
        flipped = jnp.swapaxes(block, 1, 2).reshape(9 * cc, cc)
        summed = summed + jnp.dot(patch, flipped, preferred_element_type=jnp.float32)
    grad_clips = summed.astype(jnp.bfloat16).reshape(clips.shape)
    grad_weight = reduce_weight_grad(grad_local) / jnp.sqrt(jnp.float32(count))
    return (activated, grad_clips, grad_weight)


def solution(mesh):
    dp, tm = mesh.devices.shape
    cores = 2 if tm % 2 == 0 else 1
    split = Mesh(mesh.devices.reshape(dp, tm // cores, cores), ("dp", "chip", "core"))
    return jax.shard_map(
        per_device,
        mesh=split,
        in_specs=(
            P("dp", TM, None, None, None),
            P("dp", None),
            P(),
            P("dp", TM, None, None, None),
        ),
        out_specs=(P("dp", TM, None, None, None), P("dp", TM, None, None, None), P(TM, None)),
        check_vma=False,
    )
```

```python
import functools

import jax
import jax.numpy as jnp
from jax import lax
from jax.experimental import pallas as pl
from jax.experimental.pallas import tpu as pltpu
from jax.sharding import Mesh, PartitionSpec as P

TM = ("chip", "core")


def from_behind(value, axis, steps):
    count = lax.axis_size(axis)
    leading, last = (max(0, -steps), min(count, count - steps))
    return lax.ppermute(value, axis, [(source, source + steps) for source in range(leading, last)])


def reduce_weight_grad(grad_local):
    tm = lax.axis_size("chip") * lax.axis_size("core")
    dp = lax.axis_size("dp")
    mine = lax.all_to_all(grad_local, TM, 0, 0, tiled=True).sum(axis=0)
    step = 1
    while step < dp:
        mine = mine + lax.ppermute(mine, "dp", [(i, i ^ step) for i in range(dp)])
        step *= 2
    return mine


def im2col(frames, offset, hh, ww):
    padded = jnp.pad(frames, ((0, 0), (1, 1), (1, 1), (0, 0)))
    pieces = [
        padded[:, offset(ky) : offset(ky) + hh, offset(kx) : offset(kx) + ww]
        for ky in range(3)
        for kx in range(3)
    ]
    return jnp.concatenate(pieces, axis=3).reshape(-1, 9 * frames.shape[-1])


def forward_kernel(hh, ww, nout, nfr, mask_ref, early_ref, own_ref, ahead_ref, cot_ref, w_ref, act_ref, gp_ref, gw_ref, col_ref, pad_ref, acc_ref, flat_ref):
    frame = hh * ww
    cc = own_ref.shape[1]
    taps = 9 * cc
    lead = 2 * ww
    r = lax.broadcasted_iota(jnp.int32, (frame, cc), 0)
    i = r // ww
    j = r % ww
    pad_ref[...] = jnp.zeros_like(pad_ref)
    for f in range(nout + 2):
        if f < 2:
            source = early_ref[pl.ds(f * frame, frame), :]
        elif f < nfr + 2:
            source = own_ref[pl.ds((f - 2) * frame, frame), :]
        else:
            source = ahead_ref[pl.ds((f - nfr - 2) * frame, frame), :]
        pad_ref[pl.ds(lead, frame), :] = source.astype(jnp.float32)
        for ky in range(3):
            for kx in range(3):
                dy, dx = ky - 1, kx - 1
                s = pad_ref[pl.ds(lead + dy * ww + dx, frame), :]
                valid = (i + dy >= 0) & (i + dy < hh) & (j + dx >= 0) & (j + dx < ww)
                s = jnp.where(valid, s, 0.0)
                col_ref[pl.ds(f * frame, frame), pl.ds((ky * 3 + kx) * cc, cc)] = s.astype(col_ref.dtype)
    pre = None
    for kt in range(3):
        part = jnp.dot(col_ref[pl.ds(kt * frame, nout * frame), :], w_ref[pl.ds(kt * taps, taps), :], preferred_element_type=jnp.float32)
        part = jnp.concatenate([mask_ref[kt, t] * part[t * frame : (t + 1) * frame] for t in range(nout)], axis=0)
        pre = part if pre is None else pre + part
    sig = 1.0 / (1.0 + jnp.exp(-pre))
    act_ref[...] = (pre[: nfr * frame] * sig[: nfr * frame]).astype(act_ref.dtype)
    cot = jnp.concatenate([cot_ref[...], ahead_ref[pl.ds(2 * frame, (nout - nfr) * frame), :]], axis=0).astype(jnp.float32)
    grad = (cot * sig * (1.0 + pre * (1.0 - sig))).astype(gp_ref.dtype)
    gp_ref[...] = grad
    own_grad = grad[: nfr * frame].astype(jnp.float32)
    for kt in range(3):
        scaled = jnp.concatenate([mask_ref[kt, t] * own_grad[t * frame : (t + 1) * frame] for t in range(nfr)], axis=0)
        lhs = jnp.transpose(scaled).astype(col_ref.dtype)
        acc_ref[kt] = jnp.dot(lhs, col_ref[pl.ds(kt * frame, nfr * frame), :], preferred_element_type=jnp.float32)
    for kt in range(3):
        flat_ref[pl.ds(kt * taps, taps), :] = jnp.transpose(acc_ref[kt])
    blocks, share = gw_ref.shape[0], gw_ref.shape[1]
    for b in range(blocks):
        gw_ref[b] = flat_ref[pl.ds(b * share, share), :]


def forward_call(mask, early, own, ahead, cot, w, hh, ww, nout, nfr, blocks):
    frame = hh * ww
    cc = own.shape[1]
    krows = w.shape[0]
    vmem = pl.BlockSpec(memory_space=pltpu.VMEM)
    flops = 2 * 3 * frame * 9 * cc * cc * (nout + nfr)
    return pl.pallas_call(
        functools.partial(forward_kernel, hh, ww, nout, nfr),
        out_shape=(
            jax.ShapeDtypeStruct((nfr * frame, cc), jnp.bfloat16),
            jax.ShapeDtypeStruct((nout * frame, cc), jnp.bfloat16),
            jax.ShapeDtypeStruct((blocks, krows // blocks, cc), jnp.float32),
        ),
        in_specs=[pl.BlockSpec(memory_space=pltpu.SMEM), vmem, vmem, vmem, vmem, vmem],
        out_specs=(vmem, vmem, vmem),
        scratch_shapes=[
            pltpu.VMEM(((nout + 2) * frame, 9 * cc), jnp.bfloat16),
            pltpu.VMEM((frame + 4 * ww, cc), jnp.float32),
            pltpu.VMEM((3, cc, 9 * cc), jnp.float32),
            pltpu.VMEM((krows, cc), jnp.float32),
        ],
        compiler_params=pltpu.CompilerParams(vmem_limit_bytes=48 * 1024 * 1024),
        cost_estimate=pl.CostEstimate(
            flops=flops,
            transcendentals=nout * frame * cc,
            bytes_accessed=2 * (early.size + own.size + ahead.size + cot.size + w.size) + 4 * krows * cc,
        ),
    )(mask, early, own, ahead, cot, w)


def per_device(clips, segment_ids, conv_weight, cotangent):
    nfr = clips.shape[1]
    hh = clips.shape[2]
    ww = clips.shape[3]
    cc = clips.shape[4]
    rows = nfr * hh * ww
    earlier = from_behind(clips[:, nfr - 2 :], TM, 1)[0]
    ahead = from_behind(jnp.concatenate([clips[:, :2], cotangent[:, :2]], axis=1), TM, -1)[0]
    segrow = segment_ids[0]
    segp = jnp.concatenate([jnp.full((2,), -1, jnp.int32), segrow, jnp.full((2,), -2, jnp.int32)])
    start = (lax.axis_index("chip") * lax.axis_size("core") + lax.axis_index("core")) * nfr
    seglocal = lax.dynamic_slice_in_dim(segp, start, nfr + 4, 0)
    nout = nfr + 2
    centre = seglocal[2 : 2 + nout]
    mask = jnp.stack([(seglocal[kt : kt + nout] == centre) for kt in range(3)]).astype(jnp.float32)
    tm = lax.axis_size("chip") * lax.axis_size("core")
    act, grad_pre, grad_local = forward_call(
        mask,
        earlier.reshape(-1, cc),
        clips.reshape(-1, cc),
        ahead.reshape(-1, cc),
        cotangent.reshape(-1, cc),
        conv_weight,
        hh,
        ww,
        nout,
        nfr,
        tm,
    )
    activated = act.reshape(clips.shape)
    count = lax.axis_size("dp") * (lax.axis_size("chip") * lax.axis_size("core")) * rows
    grad_ext = grad_pre.reshape(nout, hh, ww, cc)
    own = seglocal[2 : 2 + nfr]
    summed = jnp.zeros((rows, cc), jnp.float32)
    for kt in range(3):
        d = 2 - kt
        later = grad_ext[d : d + nfr]
        keep = seglocal[2 + d : 2 + d + nfr] == own
        later = jnp.where(keep[:, None, None, None], later, jnp.zeros_like(later))
        patch = im2col(later, lambda k: 2 - k, hh, ww)
        block = conv_weight[kt * 9 * cc : (kt + 1) * 9 * cc].reshape(9, cc, cc)
        flipped = jnp.swapaxes(block, 1, 2).reshape(9 * cc, cc)
        summed = summed + jnp.dot(patch, flipped, preferred_element_type=jnp.float32)
    grad_clips = summed.astype(jnp.bfloat16).reshape(clips.shape)
    grad_weight = reduce_weight_grad(grad_local) / jnp.sqrt(jnp.float32(count))
    return (activated, grad_clips, grad_weight)


def solution(mesh):
    dp, tm = mesh.devices.shape
    cores = 2 if tm % 2 == 0 else 1
    split = Mesh(mesh.devices.reshape(dp, tm // cores, cores), ("dp", "chip", "core"))
    return jax.shard_map(
        per_device,
        mesh=split,
        in_specs=(
            P("dp", TM, None, None, None),
            P("dp", None),
            P(),
            P("dp", TM, None, None, None),
        ),
        out_specs=(P("dp", TM, None, None, None), P("dp", TM, None, None, None), P(TM, None)),
        check_vma=False,
    )
```

```python
import functools

import jax
import jax.numpy as jnp
from jax import lax
from jax.experimental import pallas as pl
from jax.experimental.pallas import tpu as pltpu
from jax.sharding import Mesh, PartitionSpec as P

TM = ("chip", "core")


def from_behind(value, axis, steps):
    count = lax.axis_size(axis)
    leading, last = (max(0, -steps), min(count, count - steps))
    return lax.ppermute(value, axis, [(source, source + steps) for source in range(leading, last)])


def reduce_weight_grad(mine, other):
    dp = lax.axis_size("dp")
    cores = lax.axis_size("core")
    mine = mine + lax.ppermute(other, "core", [(i, (i + 1) % cores) for i in range(cores)])
    mine = lax.all_to_all(mine, "chip", 0, 0, tiled=True).sum(axis=0)
    step = 1
    while step < dp:
        mine = mine + lax.ppermute(mine, "dp", [(i, i ^ step) for i in range(dp)])
        step *= 2
    return mine


def im2col(frames, offset, hh, ww):
    padded = jnp.pad(frames, ((0, 0), (1, 1), (1, 1), (0, 0)))
    pieces = [
        padded[:, offset(ky) : offset(ky) + hh, offset(kx) : offset(kx) + ww]
        for ky in range(3)
        for kx in range(3)
    ]
    return jnp.concatenate(pieces, axis=3).reshape(-1, 9 * frames.shape[-1])


def forward_kernel(hh, ww, nout, nfr, core_ref, mask_ref, early_ref, own_ref, ahead_ref, cot_ref, w_ref, act_ref, gp_ref, mine_ref, other_ref, col_ref, pad_ref, acc_ref, flat_ref):
    frame = hh * ww
    cc = own_ref.shape[1]
    taps = 9 * cc
    lead = 2 * ww
    r = lax.broadcasted_iota(jnp.int32, (frame, cc), 0)
    i = r // ww
    j = r % ww
    pad_ref[...] = jnp.zeros_like(pad_ref)
    for f in range(nout + 2):
        if f < 2:
            source = early_ref[pl.ds(f * frame, frame), :]
        elif f < nfr + 2:
            source = own_ref[pl.ds((f - 2) * frame, frame), :]
        else:
            source = ahead_ref[pl.ds((f - nfr - 2) * frame, frame), :]
        pad_ref[pl.ds(lead, frame), :] = source.astype(jnp.float32)
        for ky in range(3):
            for kx in range(3):
                dy, dx = ky - 1, kx - 1
                s = pad_ref[pl.ds(lead + dy * ww + dx, frame), :]
                valid = (i + dy >= 0) & (i + dy < hh) & (j + dx >= 0) & (j + dx < ww)
                s = jnp.where(valid, s, 0.0)
                col_ref[f, :, pl.ds((ky * 3 + kx) * cc, cc)] = s.astype(col_ref.dtype)
    for t in range(nout):
        pre = jnp.zeros((frame, cc), jnp.float32)
        for kt in range(3):
            part = jnp.dot(col_ref[t + kt], w_ref[pl.ds(kt * taps, taps), :], preferred_element_type=jnp.float32)
            pre = pre + mask_ref[kt, t] * part
        sig = 1.0 / (1.0 + jnp.exp(-pre))
        if t < nfr:
            act_ref[pl.ds(t * frame, frame), :] = (pre * sig).astype(act_ref.dtype)
        if t < nfr:
            cot = cot_ref[pl.ds(t * frame, frame), :].astype(jnp.float32)
        else:
            cot = ahead_ref[pl.ds((t - nfr + 2) * frame, frame), :].astype(jnp.float32)
        gp_ref[pl.ds(t * frame, frame), :] = (cot * sig * (1.0 + pre * (1.0 - sig))).astype(gp_ref.dtype)
    acc_ref[...] = jnp.zeros_like(acc_ref)
    for t in range(nfr):
        g = gp_ref[pl.ds(t * frame, frame), :].astype(jnp.float32)
        gt = jnp.transpose(g).astype(col_ref.dtype)
        for kt in range(3):
            part = jnp.dot(gt, col_ref[t + kt], preferred_element_type=jnp.float32)
            acc_ref[kt] = acc_ref[kt] + mask_ref[kt, t] * part
    for kt in range(3):
        flat_ref[pl.ds(kt * taps, taps), :] = jnp.transpose(acc_ref[kt])
    chips, share = mine_ref.shape[0], mine_ref.shape[1]
    first = core_ref[0] == 0
    for c in range(chips):
        even = flat_ref[pl.ds(2 * c * share, share), :]
        odd = flat_ref[pl.ds((2 * c + 1) * share, share), :]
        mine_ref[c] = jnp.where(first, even, odd)
        other_ref[c] = jnp.where(first, odd, even)


def forward_call(core, mask, early, own, ahead, cot, w, hh, ww, nout, nfr, blocks):
    frame = hh * ww
    cc = own.shape[1]
    krows = w.shape[0]
    vmem = pl.BlockSpec(memory_space=pltpu.VMEM)
    flops = 2 * 3 * frame * 9 * cc * cc * (nout + nfr)
    return pl.pallas_call(
        functools.partial(forward_kernel, hh, ww, nout, nfr),
        out_shape=(
            jax.ShapeDtypeStruct((nfr * frame, cc), jnp.bfloat16),
            jax.ShapeDtypeStruct((nout * frame, cc), jnp.bfloat16),
            jax.ShapeDtypeStruct((blocks // 2, krows // blocks, cc), jnp.float32),
            jax.ShapeDtypeStruct((blocks // 2, krows // blocks, cc), jnp.float32),
        ),
        in_specs=[pl.BlockSpec(memory_space=pltpu.SMEM), pl.BlockSpec(memory_space=pltpu.SMEM), vmem, vmem, vmem, vmem, vmem],
        out_specs=(vmem, vmem, vmem, vmem),
        scratch_shapes=[
            pltpu.VMEM((nout + 2, frame, 9 * cc), jnp.bfloat16),
            pltpu.VMEM((frame + 4 * ww, cc), jnp.float32),
            pltpu.VMEM((3, cc, 9 * cc), jnp.float32),
            pltpu.VMEM((krows, cc), jnp.float32),
        ],
        compiler_params=pltpu.CompilerParams(vmem_limit_bytes=48 * 1024 * 1024),
        cost_estimate=pl.CostEstimate(
            flops=flops,
            transcendentals=nout * frame * cc,
            bytes_accessed=2 * (early.size + own.size + ahead.size + cot.size + w.size) + 4 * krows * cc,
        ),
    )(core, mask, early, own, ahead, cot, w)


def per_device(clips, segment_ids, conv_weight, cotangent):
    nfr = clips.shape[1]
    hh = clips.shape[2]
    ww = clips.shape[3]
    cc = clips.shape[4]
    rows = nfr * hh * ww
    earlier = from_behind(clips[:, nfr - 2 :], TM, 1)[0]
    ahead = from_behind(jnp.concatenate([clips[:, :2], cotangent[:, :2]], axis=1), TM, -1)[0]
    segrow = segment_ids[0]
    segp = jnp.concatenate([jnp.full((2,), -1, jnp.int32), segrow, jnp.full((2,), -2, jnp.int32)])
    start = (lax.axis_index("chip") * lax.axis_size("core") + lax.axis_index("core")) * nfr
    seglocal = lax.dynamic_slice_in_dim(segp, start, nfr + 4, 0)
    nout = nfr + 2
    centre = seglocal[2 : 2 + nout]
    mask = jnp.stack([(seglocal[kt : kt + nout] == centre) for kt in range(3)]).astype(jnp.float32)
    tm = lax.axis_size("chip") * lax.axis_size("core")
    core = lax.axis_index("core").astype(jnp.int32).reshape(1)
    act, grad_pre, mine, other = forward_call(
        core,
        mask,
        earlier.reshape(-1, cc),
        clips.reshape(-1, cc),
        ahead.reshape(-1, cc),
        cotangent.reshape(-1, cc),
        conv_weight,
        hh,
        ww,
        nout,
        nfr,
        tm,
    )
    activated = act.reshape(clips.shape)
    count = lax.axis_size("dp") * (lax.axis_size("chip") * lax.axis_size("core")) * rows
    grad_ext = grad_pre.reshape(nout, hh, ww, cc)
    own = seglocal[2 : 2 + nfr]
    summed = jnp.zeros((rows, cc), jnp.float32)
    for kt in range(3):
        d = 2 - kt
        later = grad_ext[d : d + nfr]
        keep = seglocal[2 + d : 2 + d + nfr] == own
        later = jnp.where(keep[:, None, None, None], later, jnp.zeros_like(later))
        patch = im2col(later, lambda k: 2 - k, hh, ww)
        block = conv_weight[kt * 9 * cc : (kt + 1) * 9 * cc].reshape(9, cc, cc)
        flipped = jnp.swapaxes(block, 1, 2).reshape(9 * cc, cc)
        summed = summed + jnp.dot(patch, flipped, preferred_element_type=jnp.float32)
    grad_clips = summed.astype(jnp.bfloat16).reshape(clips.shape)
    grad_weight = reduce_weight_grad(mine, other) / jnp.sqrt(jnp.float32(count))
    return (activated, grad_clips, grad_weight)


def solution(mesh):
    dp, tm = mesh.devices.shape
    cores = 2 if tm % 2 == 0 else 1
    split = Mesh(mesh.devices.reshape(dp, tm // cores, cores), ("dp", "chip", "core"))
    return jax.shard_map(
        per_device,
        mesh=split,
        in_specs=(
            P("dp", TM, None, None, None),
            P("dp", None),
            P(),
            P("dp", TM, None, None, None),
        ),
        out_specs=(P("dp", TM, None, None, None), P("dp", TM, None, None, None), P(TM, None)),
        check_vma=False,
    )
```

```python
import functools

import jax
import jax.numpy as jnp
from jax import lax
from jax.experimental import pallas as pl
from jax.experimental.pallas import tpu as pltpu
from jax.sharding import Mesh, PartitionSpec as P

TM = ("chip", "core")


def from_behind(value, axis, steps):
    count = lax.axis_size(axis)
    leading, last = (max(0, -steps), min(count, count - steps))
    return lax.ppermute(value, axis, [(source, source + steps) for source in range(leading, last)])


def reduce_weight_grad(mine, other):
    dp = lax.axis_size("dp")
    cores = lax.axis_size("core")
    mine = mine + lax.ppermute(other, "core", [(i, (i + 1) % cores) for i in range(cores)])
    mine = lax.all_to_all(mine, "chip", 0, 0, tiled=True).sum(axis=0)
    step = dp // 2
    while step >= 1:
        mine = mine + lax.ppermute(mine, "dp", [(i, i ^ step) for i in range(dp)])
        step //= 2
    return mine


def im2col(frames, offset, hh, ww):
    padded = jnp.pad(frames, ((0, 0), (1, 1), (1, 1), (0, 0)))
    pieces = [
        padded[:, offset(ky) : offset(ky) + hh, offset(kx) : offset(kx) + ww]
        for ky in range(3)
        for kx in range(3)
    ]
    return jnp.concatenate(pieces, axis=3).reshape(-1, 9 * frames.shape[-1])


def forward_kernel(hh, ww, nout, nfr, core_ref, mask_ref, early_ref, own_ref, ahead_ref, cot_ref, w_ref, act_ref, gp_ref, mine_ref, other_ref, col_ref, pad_ref, acc_ref, flat_ref):
    frame = hh * ww
    cc = own_ref.shape[1]
    taps = 9 * cc
    lead = 2 * ww
    r = lax.broadcasted_iota(jnp.int32, (frame, cc), 0)
    i = r // ww
    j = r % ww
    pad_ref[...] = jnp.zeros_like(pad_ref)
    for f in range(nout + 2):
        if f < 2:
            source = early_ref[pl.ds(f * frame, frame), :]
        elif f < nfr + 2:
            source = own_ref[pl.ds((f - 2) * frame, frame), :]
        else:
            source = ahead_ref[pl.ds((f - nfr - 2) * frame, frame), :]
        pad_ref[pl.ds(lead, frame), :] = source.astype(jnp.float32)
        for ky in range(3):
            for kx in range(3):
                dy, dx = ky - 1, kx - 1
                s = pad_ref[pl.ds(lead + dy * ww + dx, frame), :]
                valid = (i + dy >= 0) & (i + dy < hh) & (j + dx >= 0) & (j + dx < ww)
                s = jnp.where(valid, s, 0.0)
                col_ref[f, :, pl.ds((ky * 3 + kx) * cc, cc)] = s.astype(col_ref.dtype)
    for t in range(nout):
        pre = jnp.zeros((frame, cc), jnp.float32)
        for kt in range(3):
            part = jnp.dot(col_ref[t + kt], w_ref[pl.ds(kt * taps, taps), :], preferred_element_type=jnp.float32)
            pre = pre + mask_ref[kt, t] * part
        sig = 1.0 / (1.0 + jnp.exp(-pre))
        if t < nfr:
            act_ref[pl.ds(t * frame, frame), :] = (pre * sig).astype(act_ref.dtype)
        if t < nfr:
            cot = cot_ref[pl.ds(t * frame, frame), :].astype(jnp.float32)
        else:
            cot = ahead_ref[pl.ds((t - nfr + 2) * frame, frame), :].astype(jnp.float32)
        gp_ref[pl.ds(t * frame, frame), :] = (cot * sig * (1.0 + pre * (1.0 - sig))).astype(gp_ref.dtype)
    acc_ref[...] = jnp.zeros_like(acc_ref)
    for t in range(nfr):
        g = gp_ref[pl.ds(t * frame, frame), :].astype(jnp.float32)
        gt = jnp.transpose(g).astype(col_ref.dtype)
        for kt in range(3):
            part = jnp.dot(gt, col_ref[t + kt], preferred_element_type=jnp.float32)
            acc_ref[kt] = acc_ref[kt] + mask_ref[kt, t] * part
    for kt in range(3):
        flat_ref[pl.ds(kt * taps, taps), :] = jnp.transpose(acc_ref[kt])
    chips, share = mine_ref.shape[0], mine_ref.shape[1]
    first = core_ref[0] == 0
    for c in range(chips):
        even = flat_ref[pl.ds(2 * c * share, share), :]
        odd = flat_ref[pl.ds((2 * c + 1) * share, share), :]
        mine_ref[c] = jnp.where(first, even, odd)
        other_ref[c] = jnp.where(first, odd, even)


def forward_call(core, mask, early, own, ahead, cot, w, hh, ww, nout, nfr, blocks):
    frame = hh * ww
    cc = own.shape[1]
    krows = w.shape[0]
    vmem = pl.BlockSpec(memory_space=pltpu.VMEM)
    flops = 2 * 3 * frame * 9 * cc * cc * (nout + nfr)
    return pl.pallas_call(
        functools.partial(forward_kernel, hh, ww, nout, nfr),
        out_shape=(
            jax.ShapeDtypeStruct((nfr * frame, cc), jnp.bfloat16),
            jax.ShapeDtypeStruct((nout * frame, cc), jnp.bfloat16),
            jax.ShapeDtypeStruct((blocks // 2, krows // blocks, cc), jnp.float32),
            jax.ShapeDtypeStruct((blocks // 2, krows // blocks, cc), jnp.float32),
        ),
        in_specs=[pl.BlockSpec(memory_space=pltpu.SMEM), pl.BlockSpec(memory_space=pltpu.SMEM), vmem, vmem, vmem, vmem, vmem],
        out_specs=(vmem, vmem, vmem, vmem),
        scratch_shapes=[
            pltpu.VMEM((nout + 2, frame, 9 * cc), jnp.bfloat16),
            pltpu.VMEM((frame + 4 * ww, cc), jnp.float32),
            pltpu.VMEM((3, cc, 9 * cc), jnp.float32),
            pltpu.VMEM((krows, cc), jnp.float32),
        ],
        compiler_params=pltpu.CompilerParams(vmem_limit_bytes=48 * 1024 * 1024),
        cost_estimate=pl.CostEstimate(
            flops=flops,
            transcendentals=nout * frame * cc,
            bytes_accessed=2 * (early.size + own.size + ahead.size + cot.size + w.size) + 4 * krows * cc,
        ),
    )(core, mask, early, own, ahead, cot, w)


def per_device(clips, segment_ids, conv_weight, cotangent):
    nfr = clips.shape[1]
    hh = clips.shape[2]
    ww = clips.shape[3]
    cc = clips.shape[4]
    rows = nfr * hh * ww
    earlier = from_behind(clips[:, nfr - 2 :], TM, 1)[0]
    ahead = from_behind(jnp.concatenate([clips[:, :2], cotangent[:, :2]], axis=1), TM, -1)[0]
    segrow = segment_ids[0]
    segp = jnp.concatenate([jnp.full((2,), -1, jnp.int32), segrow, jnp.full((2,), -2, jnp.int32)])
    start = (lax.axis_index("chip") * lax.axis_size("core") + lax.axis_index("core")) * nfr
    seglocal = lax.dynamic_slice_in_dim(segp, start, nfr + 4, 0)
    nout = nfr + 2
    centre = seglocal[2 : 2 + nout]
    mask = jnp.stack([(seglocal[kt : kt + nout] == centre) for kt in range(3)]).astype(jnp.float32)
    tm = lax.axis_size("chip") * lax.axis_size("core")
    core = lax.axis_index("core").astype(jnp.int32).reshape(1)
    act, grad_pre, mine, other = forward_call(
        core,
        mask,
        earlier.reshape(-1, cc),
        clips.reshape(-1, cc),
        ahead.reshape(-1, cc),
        cotangent.reshape(-1, cc),
        conv_weight,
        hh,
        ww,
        nout,
        nfr,
        tm,
    )
    activated = act.reshape(clips.shape)
    count = lax.axis_size("dp") * (lax.axis_size("chip") * lax.axis_size("core")) * rows
    grad_ext = grad_pre.reshape(nout, hh, ww, cc)
    own = seglocal[2 : 2 + nfr]
    summed = jnp.zeros((rows, cc), jnp.float32)
    for kt in range(3):
        d = 2 - kt
        later = grad_ext[d : d + nfr]
        keep = seglocal[2 + d : 2 + d + nfr] == own
        later = jnp.where(keep[:, None, None, None], later, jnp.zeros_like(later))
        patch = im2col(later, lambda k: 2 - k, hh, ww)
        block = conv_weight[kt * 9 * cc : (kt + 1) * 9 * cc].reshape(9, cc, cc)
        flipped = jnp.swapaxes(block, 1, 2).reshape(9 * cc, cc)
        summed = summed + jnp.dot(patch, flipped, preferred_element_type=jnp.float32)
    grad_clips = summed.astype(jnp.bfloat16).reshape(clips.shape)
    grad_weight = reduce_weight_grad(mine, other) / jnp.sqrt(jnp.float32(count))
    return (activated, grad_clips, grad_weight)


def solution(mesh):
    dp, tm = mesh.devices.shape
    cores = 2 if tm % 2 == 0 else 1
    split = Mesh(mesh.devices.reshape(dp, tm // cores, cores), ("dp", "chip", "core"))
    return jax.shard_map(
        per_device,
        mesh=split,
        in_specs=(
            P("dp", TM, None, None, None),
            P("dp", None),
            P(),
            P("dp", TM, None, None, None),
        ),
        out_specs=(P("dp", TM, None, None, None), P("dp", TM, None, None, None), P(TM, None)),
        check_vma=False,
    )
```

```python
import functools

import jax
import jax.numpy as jnp
from jax import lax
from jax.experimental import pallas as pl
from jax.experimental.pallas import tpu as pltpu
from jax.sharding import Mesh, PartitionSpec as P

TM = ("chip", "core")


def from_behind(value, axis, steps):
    count = lax.axis_size(axis)
    leading, last = (max(0, -steps), min(count, count - steps))
    return lax.ppermute(value, axis, [(source, source + steps) for source in range(leading, last)])


def reduce_weight_grad(mine, other):
    dp = lax.axis_size("dp")
    cores = lax.axis_size("core")
    mine = mine + lax.ppermute(other, "core", [(i, (i + 1) % cores) for i in range(cores)])
    mine = lax.all_to_all(mine, "chip", 0, 0, tiled=True).sum(axis=0)
    step = 1
    while step < dp:
        mine = mine + lax.ppermute(mine, "dp", [(i, i ^ step) for i in range(dp)])
        step *= 2
    return mine


def im2col(frames, offset, hh, ww):
    padded = jnp.pad(frames, ((0, 0), (1, 1), (1, 1), (0, 0)))
    pieces = [
        padded[:, offset(ky) : offset(ky) + hh, offset(kx) : offset(kx) + ww]
        for ky in range(3)
        for kx in range(3)
    ]
    return jnp.concatenate(pieces, axis=3).reshape(-1, 9 * frames.shape[-1])


def forward_kernel(hh, ww, nout, nfr, core_ref, mask_ref, early_ref, own_ref, ahead_ref, cot_ref, w_ref, act_ref, gp_ref, mine_ref, other_ref, col_ref, pad_ref, acc_ref, flat_ref):
    frame = hh * ww
    cc = own_ref.shape[1]
    taps = 9 * cc
    lead = 2 * ww
    r = lax.broadcasted_iota(jnp.int32, (frame, cc), 0)
    i = r // ww
    j = r % ww
    pad_ref[...] = jnp.zeros_like(pad_ref)
    for f in range(nout + 2):
        if f < 2:
            source = early_ref[pl.ds((f + nfr - 2) * frame, frame), :]
        elif f < nfr + 2:
            source = own_ref[pl.ds((f - 2) * frame, frame), :]
        else:
            source = ahead_ref[pl.ds((f - nfr - 2) * frame, frame), :]
        pad_ref[pl.ds(lead, frame), :] = source.astype(jnp.float32)
        for ky in range(3):
            for kx in range(3):
                dy, dx = ky - 1, kx - 1
                s = pad_ref[pl.ds(lead + dy * ww + dx, frame), :]
                valid = (i + dy >= 0) & (i + dy < hh) & (j + dx >= 0) & (j + dx < ww)
                s = jnp.where(valid, s, 0.0)
                col_ref[f, :, pl.ds((ky * 3 + kx) * cc, cc)] = s.astype(col_ref.dtype)
    for t in range(nout):
        pre = jnp.zeros((frame, cc), jnp.float32)
        for kt in range(3):
            part = jnp.dot(col_ref[t + kt], w_ref[pl.ds(kt * taps, taps), :], preferred_element_type=jnp.float32)
            pre = pre + mask_ref[kt, t] * part
        sig = 1.0 / (1.0 + jnp.exp(-pre))
        if t < nfr:
            act_ref[pl.ds(t * frame, frame), :] = (pre * sig).astype(act_ref.dtype)
        if t < nfr:
            cot = cot_ref[pl.ds(t * frame, frame), :].astype(jnp.float32)
        else:
            cot = ahead_ref[pl.ds((t - nfr + 2) * frame, frame), :].astype(jnp.float32)
        gp_ref[pl.ds(t * frame, frame), :] = (cot * sig * (1.0 + pre * (1.0 - sig))).astype(gp_ref.dtype)
    acc_ref[...] = jnp.zeros_like(acc_ref)
    for t in range(nfr):
        g = gp_ref[pl.ds(t * frame, frame), :].astype(jnp.float32)
        gt = jnp.transpose(g).astype(col_ref.dtype)
        for kt in range(3):
            part = jnp.dot(gt, col_ref[t + kt], preferred_element_type=jnp.float32)
            acc_ref[kt] = acc_ref[kt] + mask_ref[kt, t] * part
    for kt in range(3):
        flat_ref[pl.ds(kt * taps, taps), :] = jnp.transpose(acc_ref[kt])
    chips, share = mine_ref.shape[0], mine_ref.shape[1]
    first = core_ref[0] == 0
    for c in range(chips):
        even = flat_ref[pl.ds(2 * c * share, share), :]
        odd = flat_ref[pl.ds((2 * c + 1) * share, share), :]
        mine_ref[c] = jnp.where(first, even, odd)
        other_ref[c] = jnp.where(first, odd, even)


def forward_call(core, mask, early, own, ahead, cot, w, hh, ww, nout, nfr, blocks):
    frame = hh * ww
    cc = own.shape[1]
    krows = w.shape[0]
    vmem = pl.BlockSpec(memory_space=pltpu.VMEM)
    flops = 2 * 3 * frame * 9 * cc * cc * (nout + nfr)
    return pl.pallas_call(
        functools.partial(forward_kernel, hh, ww, nout, nfr),
        out_shape=(
            jax.ShapeDtypeStruct((nfr * frame, cc), jnp.bfloat16),
            jax.ShapeDtypeStruct((nout * frame, cc), jnp.bfloat16),
            jax.ShapeDtypeStruct((blocks // 2, krows // blocks, cc), jnp.float32),
            jax.ShapeDtypeStruct((blocks // 2, krows // blocks, cc), jnp.float32),
        ),
        in_specs=[pl.BlockSpec(memory_space=pltpu.SMEM), pl.BlockSpec(memory_space=pltpu.SMEM), vmem, vmem, vmem, vmem, vmem],
        out_specs=(vmem, vmem, vmem, vmem),
        scratch_shapes=[
            pltpu.VMEM((nout + 2, frame, 9 * cc), jnp.bfloat16),
            pltpu.VMEM((frame + 4 * ww, cc), jnp.float32),
            pltpu.VMEM((3, cc, 9 * cc), jnp.float32),
            pltpu.VMEM((krows, cc), jnp.float32),
        ],
        compiler_params=pltpu.CompilerParams(vmem_limit_bytes=48 * 1024 * 1024),
        cost_estimate=pl.CostEstimate(
            flops=flops,
            transcendentals=nout * frame * cc,
            bytes_accessed=2 * (early.size + own.size + ahead.size + cot.size + w.size) + 4 * krows * cc,
        ),
    )(core, mask, early, own, ahead, cot, w)


def per_device(clips, segment_ids, conv_weight, cotangent):
    nfr = clips.shape[1]
    hh = clips.shape[2]
    ww = clips.shape[3]
    cc = clips.shape[4]
    rows = nfr * hh * ww
    earlier = from_behind(clips, TM, 1)[0]
    ahead = from_behind(jnp.concatenate([clips[:, :2], cotangent[:, :2]], axis=1), TM, -1)[0]
    segrow = segment_ids[0]
    segp = jnp.concatenate([jnp.full((2,), -1, jnp.int32), segrow, jnp.full((2,), -2, jnp.int32)])
    start = (lax.axis_index("chip") * lax.axis_size("core") + lax.axis_index("core")) * nfr
    seglocal = lax.dynamic_slice_in_dim(segp, start, nfr + 4, 0)
    nout = nfr + 2
    centre = seglocal[2 : 2 + nout]
    mask = jnp.stack([(seglocal[kt : kt + nout] == centre) for kt in range(3)]).astype(jnp.float32)
    tm = lax.axis_size("chip") * lax.axis_size("core")
    core = lax.axis_index("core").astype(jnp.int32).reshape(1)
    act, grad_pre, mine, other = forward_call(
        core,
        mask,
        earlier.reshape(-1, cc),
        clips.reshape(-1, cc),
        ahead.reshape(-1, cc),
        cotangent.reshape(-1, cc),
        conv_weight,
        hh,
        ww,
        nout,
        nfr,
        tm,
    )
    activated = act.reshape(clips.shape)
    count = lax.axis_size("dp") * (lax.axis_size("chip") * lax.axis_size("core")) * rows
    grad_ext = grad_pre.reshape(nout, hh, ww, cc)
    own = seglocal[2 : 2 + nfr]
    summed = jnp.zeros((rows, cc), jnp.float32)
    for kt in range(3):
        d = 2 - kt
        later = grad_ext[d : d + nfr]
        keep = seglocal[2 + d : 2 + d + nfr] == own
        later = jnp.where(keep[:, None, None, None], later, jnp.zeros_like(later))
        patch = im2col(later, lambda k: 2 - k, hh, ww)
        block = conv_weight[kt * 9 * cc : (kt + 1) * 9 * cc].reshape(9, cc, cc)
        flipped = jnp.swapaxes(block, 1, 2).reshape(9 * cc, cc)
        summed = summed + jnp.dot(patch, flipped, preferred_element_type=jnp.float32)
    grad_clips = summed.astype(jnp.bfloat16).reshape(clips.shape)
    grad_weight = reduce_weight_grad(mine, other) / jnp.sqrt(jnp.float32(count))
    return (activated, grad_clips, grad_weight)


def solution(mesh):
    dp, tm = mesh.devices.shape
    cores = 2 if tm % 2 == 0 else 1
    split = Mesh(mesh.devices.reshape(dp, tm // cores, cores), ("dp", "chip", "core"))
    return jax.shard_map(
        per_device,
        mesh=split,
        in_specs=(
            P("dp", TM, None, None, None),
            P("dp", None),
            P(),
            P("dp", TM, None, None, None),
        ),
        out_specs=(P("dp", TM, None, None, None), P("dp", TM, None, None, None), P(TM, None)),
        check_vma=False,
    )
```

```python
import functools

import jax
import jax.numpy as jnp
from jax import lax
from jax.experimental import pallas as pl
from jax.experimental.pallas import tpu as pltpu
from jax.sharding import Mesh, PartitionSpec as P

TM = ("chip", "core")


def from_behind(value, axis, steps):
    count = lax.axis_size(axis)
    leading, last = (max(0, -steps), min(count, count - steps))
    return lax.ppermute(value, axis, [(source, source + steps) for source in range(leading, last)])


def reduce_weight_grad(mine, other):
    dp = lax.axis_size("dp")
    cores = lax.axis_size("core")
    mine = mine + lax.ppermute(other, "core", [(i, (i + 1) % cores) for i in range(cores)])
    mine = lax.all_to_all(mine, "chip", 0, 0, tiled=True).sum(axis=0)
    step = 1
    while step < dp:
        mine = mine + lax.ppermute(mine, "dp", [(i, i ^ step) for i in range(dp)])
        step *= 2
    return mine


def im2col(frames, offset, hh, ww):
    padded = jnp.pad(frames, ((0, 0), (1, 1), (1, 1), (0, 0)))
    pieces = [
        padded[:, offset(ky) : offset(ky) + hh, offset(kx) : offset(kx) + ww]
        for ky in range(3)
        for kx in range(3)
    ]
    return jnp.concatenate(pieces, axis=3).reshape(-1, 9 * frames.shape[-1])


def forward_kernel(hh, ww, nout, nfr, core_ref, mask_ref, early_ref, own_ref, ahead_ref, cot_ref, w_ref, act_ref, gp_ref, mine_ref, other_ref, col_ref, pad_ref, acc_ref, flat_ref):
    frame = hh * ww
    cc = own_ref.shape[1]
    taps = 9 * cc
    lead = 2 * ww
    r = lax.broadcasted_iota(jnp.int32, (frame, cc), 0)
    i = r // ww
    j = r % ww
    pad_ref[...] = jnp.zeros_like(pad_ref)
    for f in range(nout + 2):
        if f < 2:
            source = early_ref[pl.ds(f * frame, frame), :]
        elif f < nfr + 2:
            source = own_ref[pl.ds((f - 2) * frame, frame), :]
        else:
            source = ahead_ref[pl.ds((f - nfr - 2) * frame, frame), :]
        pad_ref[pl.ds(lead, frame), :] = source.astype(jnp.float32)
        for ky in range(3):
            for kx in range(3):
                dy, dx = ky - 1, kx - 1
                s = pad_ref[pl.ds(lead + dy * ww + dx, frame), :]
                valid = (i + dy >= 0) & (i + dy < hh) & (j + dx >= 0) & (j + dx < ww)
                s = jnp.where(valid, s, 0.0)
                col_ref[f, :, pl.ds((ky * 3 + kx) * cc, cc)] = s.astype(col_ref.dtype)
    for t in range(nout):
        pre = jnp.zeros((frame, cc), jnp.float32)
        for kt in range(3):
            part = jnp.dot(col_ref[t + kt], w_ref[pl.ds(kt * taps, taps), :], preferred_element_type=jnp.float32)
            pre = pre + mask_ref[kt, t] * part
        sig = 1.0 / (1.0 + jnp.exp(-pre))
        if t < nfr:
            act_ref[pl.ds(t * frame, frame), :] = (pre * sig).astype(act_ref.dtype)
        if t < nfr:
            cot = cot_ref[pl.ds(t * frame, frame), :].astype(jnp.float32)
        else:
            cot = ahead_ref[pl.ds((t - nfr + 2) * frame, frame), :].astype(jnp.float32)
        gp_ref[pl.ds(t * frame, frame), :] = (cot * sig * (1.0 + pre * (1.0 - sig))).astype(gp_ref.dtype)
    acc_ref[...] = jnp.zeros_like(acc_ref)
    for t in range(nfr):
        g = gp_ref[pl.ds(t * frame, frame), :].astype(jnp.float32)
        gt = jnp.transpose(g).astype(col_ref.dtype)
        for kt in range(3):
            part = jnp.dot(gt, col_ref[t + kt], preferred_element_type=jnp.float32)
            acc_ref[kt] = acc_ref[kt] + mask_ref[kt, t] * part
    for kt in range(3):
        flat_ref[pl.ds(kt * taps, taps), :] = jnp.transpose(acc_ref[kt])
    chips, share = mine_ref.shape[0], mine_ref.shape[1]
    first = core_ref[0] == 0
    for c in range(chips):
        even = flat_ref[pl.ds(2 * c * share, share), :]
        odd = flat_ref[pl.ds((2 * c + 1) * share, share), :]
        mine_ref[c] = jnp.where(first, even, odd)
        other_ref[c] = jnp.where(first, odd, even)


def forward_call(core, mask, early, own, ahead, cot, w, hh, ww, nout, nfr, blocks):
    frame = hh * ww
    cc = own.shape[1]
    krows = w.shape[0]
    vmem = pl.BlockSpec(memory_space=pltpu.VMEM)
    flops = 2 * 3 * frame * 9 * cc * cc * (nout + nfr)
    return pl.pallas_call(
        functools.partial(forward_kernel, hh, ww, nout, nfr),
        out_shape=(
            jax.ShapeDtypeStruct((nfr * frame, cc), jnp.bfloat16),
            jax.ShapeDtypeStruct((nout * frame, cc), jnp.bfloat16),
            jax.ShapeDtypeStruct((blocks // 2, krows // blocks, cc), jnp.float32),
            jax.ShapeDtypeStruct((blocks // 2, krows // blocks, cc), jnp.float32),
        ),
        in_specs=[pl.BlockSpec(memory_space=pltpu.SMEM), pl.BlockSpec(memory_space=pltpu.SMEM), vmem, vmem, vmem, vmem, vmem],
        out_specs=(vmem, vmem, vmem, vmem),
        scratch_shapes=[
            pltpu.VMEM((nout + 2, frame, 9 * cc), jnp.bfloat16),
            pltpu.VMEM((frame + 4 * ww, cc), jnp.float32),
            pltpu.VMEM((3, cc, 9 * cc), jnp.float32),
            pltpu.VMEM((krows, cc), jnp.float32),
        ],
        compiler_params=pltpu.CompilerParams(vmem_limit_bytes=48 * 1024 * 1024),
        cost_estimate=pl.CostEstimate(
            flops=flops,
            transcendentals=nout * frame * cc,
            bytes_accessed=2 * (early.size + own.size + ahead.size + cot.size + w.size) + 4 * krows * cc,
        ),
    )(core, mask, early, own, ahead, cot, w)


def input_grad_kernel(hh, ww, nfr, mask_ref, gp_ref, w_ref, out_ref, col_ref, pad_ref):
    frame = hh * ww
    cc = gp_ref.shape[1]
    lead = 2 * ww
    r = lax.broadcasted_iota(jnp.int32, (frame, cc), 0)
    i = r // ww
    j = r % ww
    pad_ref[...] = jnp.zeros_like(pad_ref)
    for f in range(nfr + 2):
        pad_ref[pl.ds(lead, frame), :] = gp_ref[pl.ds(f * frame, frame), :].astype(jnp.float32)
        for ky in range(3):
            for kx in range(3):
                dy, dx = 1 - ky, 1 - kx
                s = pad_ref[pl.ds(lead + dy * ww + dx, frame), :]
                valid = (i + dy >= 0) & (i + dy < hh) & (j + dx >= 0) & (j + dx < ww)
                s = jnp.where(valid, s, 0.0)
                col_ref[f, :, pl.ds((ky * 3 + kx) * cc, cc)] = s.astype(col_ref.dtype)
    taps = 9 * cc
    for t in range(nfr):
        acc = jnp.zeros((frame, cc), jnp.float32)
        for kt in range(3):
            part = jnp.dot(col_ref[t + 2 - kt], w_ref[pl.ds(kt * taps, taps), :], preferred_element_type=jnp.float32)
            acc = acc + mask_ref[kt, t] * part
        out_ref[pl.ds(t * frame, frame), :] = acc.astype(out_ref.dtype)


def input_grad_call(mask, gp, w, hh, ww, nfr):
    frame = hh * ww
    cc = gp.shape[1]
    vmem = pl.BlockSpec(memory_space=pltpu.VMEM)
    return pl.pallas_call(
        functools.partial(input_grad_kernel, hh, ww, nfr),
        out_shape=jax.ShapeDtypeStruct((nfr * frame, cc), jnp.bfloat16),
        in_specs=[pl.BlockSpec(memory_space=pltpu.SMEM), vmem, vmem],
        out_specs=vmem,
        scratch_shapes=[
            pltpu.VMEM((nfr + 2, frame, 9 * cc), jnp.bfloat16),
            pltpu.VMEM((frame + 4 * ww, cc), jnp.float32),
        ],
        compiler_params=pltpu.CompilerParams(vmem_limit_bytes=32 * 1024 * 1024),
        cost_estimate=pl.CostEstimate(
            flops=2 * 3 * frame * 9 * cc * cc * nfr, transcendentals=0, bytes_accessed=2 * (gp.size + w.size) + 2 * nfr * frame * cc
        ),
    )(mask, gp, w)


def per_device(clips, segment_ids, conv_weight, cotangent):
    nfr = clips.shape[1]
    hh = clips.shape[2]
    ww = clips.shape[3]
    cc = clips.shape[4]
    rows = nfr * hh * ww
    earlier = from_behind(clips[:, nfr - 2 :], TM, 1)[0]
    ahead = from_behind(jnp.concatenate([clips[:, :2], cotangent[:, :2]], axis=1), TM, -1)[0]
    segrow = segment_ids[0]
    segp = jnp.concatenate([jnp.full((2,), -1, jnp.int32), segrow, jnp.full((2,), -2, jnp.int32)])
    start = (lax.axis_index("chip") * lax.axis_size("core") + lax.axis_index("core")) * nfr
    seglocal = lax.dynamic_slice_in_dim(segp, start, nfr + 4, 0)
    nout = nfr + 2
    centre = seglocal[2 : 2 + nout]
    mask = jnp.stack([(seglocal[kt : kt + nout] == centre) for kt in range(3)]).astype(jnp.float32)
    tm = lax.axis_size("chip") * lax.axis_size("core")
    core = lax.axis_index("core").astype(jnp.int32).reshape(1)
    act, grad_pre, mine, other = forward_call(
        core,
        mask,
        earlier.reshape(-1, cc),
        clips.reshape(-1, cc),
        ahead.reshape(-1, cc),
        cotangent.reshape(-1, cc),
        conv_weight,
        hh,
        ww,
        nout,
        nfr,
        tm,
    )
    activated = act.reshape(clips.shape)
    count = lax.axis_size("dp") * (lax.axis_size("chip") * lax.axis_size("core")) * rows
    own = seglocal[2 : 2 + nfr]
    later_mask = jnp.stack([(seglocal[4 - kt : 4 - kt + nfr] == own) for kt in range(3)]).astype(jnp.float32)
    flipped = jnp.concatenate(
        [jnp.swapaxes(conv_weight[kt * 9 * cc : (kt + 1) * 9 * cc].reshape(9, cc, cc), 1, 2).reshape(9 * cc, cc) for kt in range(3)],
        axis=0,
    )
    grad_clips = input_grad_call(later_mask, grad_pre, flipped, hh, ww, nfr).reshape(clips.shape)
    grad_weight = reduce_weight_grad(mine, other) / jnp.sqrt(jnp.float32(count))
    return (activated, grad_clips, grad_weight)


def solution(mesh):
    dp, tm = mesh.devices.shape
    cores = 2 if tm % 2 == 0 else 1
    split = Mesh(mesh.devices.reshape(dp, tm // cores, cores), ("dp", "chip", "core"))
    return jax.shard_map(
        per_device,
        mesh=split,
        in_specs=(
            P("dp", TM, None, None, None),
            P("dp", None),
            P(),
            P("dp", TM, None, None, None),
        ),
        out_specs=(P("dp", TM, None, None, None), P("dp", TM, None, None, None), P(TM, None)),
        check_vma=False,
    )
```

```python
import functools

import jax
import jax.numpy as jnp
from jax import lax
from jax.experimental import pallas as pl
from jax.experimental.pallas import tpu as pltpu
from jax.sharding import Mesh, PartitionSpec as P

TM = ("chip", "core")


def from_behind(value, axis, steps):
    count = lax.axis_size(axis)
    leading, last = (max(0, -steps), min(count, count - steps))
    return lax.ppermute(value, axis, [(source, source + steps) for source in range(leading, last)])


def reduce_weight_grad(mine, other, tie):
    dp = lax.axis_size("dp")
    cores = lax.axis_size("core")
    mine = mine + lax.ppermute(other, "core", [(i, (i + 1) % cores) for i in range(cores)])
    mine = lax.all_to_all(mine, "chip", 0, 0, tiled=True).sum(axis=0)
    mine, tie = lax.optimization_barrier((mine, tie))
    step = 1
    while step < dp:
        mine = mine + lax.ppermute(mine, "dp", [(i, i ^ step) for i in range(dp)])
        step *= 2
    return mine, tie


def im2col(frames, offset, hh, ww):
    padded = jnp.pad(frames, ((0, 0), (1, 1), (1, 1), (0, 0)))
    pieces = [
        padded[:, offset(ky) : offset(ky) + hh, offset(kx) : offset(kx) + ww]
        for ky in range(3)
        for kx in range(3)
    ]
    return jnp.concatenate(pieces, axis=3).reshape(-1, 9 * frames.shape[-1])


def forward_kernel(hh, ww, nout, nfr, core_ref, mask_ref, early_ref, own_ref, ahead_ref, cot_ref, w_ref, act_ref, gp_ref, mine_ref, other_ref, col_ref, pad_ref, acc_ref, flat_ref):
    frame = hh * ww
    cc = own_ref.shape[1]
    taps = 9 * cc
    lead = 2 * ww
    r = lax.broadcasted_iota(jnp.int32, (frame, cc), 0)
    i = r // ww
    j = r % ww
    pad_ref[...] = jnp.zeros_like(pad_ref)
    for f in range(nout + 2):
        if f < 2:
            source = early_ref[pl.ds(f * frame, frame), :]
        elif f < nfr + 2:
            source = own_ref[pl.ds((f - 2) * frame, frame), :]
        else:
            source = ahead_ref[pl.ds((f - nfr - 2) * frame, frame), :]
        pad_ref[pl.ds(lead, frame), :] = source.astype(jnp.float32)
        for ky in range(3):
            for kx in range(3):
                dy, dx = ky - 1, kx - 1
                s = pad_ref[pl.ds(lead + dy * ww + dx, frame), :]
                valid = (i + dy >= 0) & (i + dy < hh) & (j + dx >= 0) & (j + dx < ww)
                s = jnp.where(valid, s, 0.0)
                col_ref[f, :, pl.ds((ky * 3 + kx) * cc, cc)] = s.astype(col_ref.dtype)
    for t in range(nout):
        pre = jnp.zeros((frame, cc), jnp.float32)
        for kt in range(3):
            part = jnp.dot(col_ref[t + kt], w_ref[pl.ds(kt * taps, taps), :], preferred_element_type=jnp.float32)
            pre = pre + mask_ref[kt, t] * part
        sig = 1.0 / (1.0 + jnp.exp(-pre))
        if t < nfr:
            act_ref[pl.ds(t * frame, frame), :] = (pre * sig).astype(act_ref.dtype)
        if t < nfr:
            cot = cot_ref[pl.ds(t * frame, frame), :].astype(jnp.float32)
        else:
            cot = ahead_ref[pl.ds((t - nfr + 2) * frame, frame), :].astype(jnp.float32)
        gp_ref[pl.ds(t * frame, frame), :] = (cot * sig * (1.0 + pre * (1.0 - sig))).astype(gp_ref.dtype)
    acc_ref[...] = jnp.zeros_like(acc_ref)
    for t in range(nfr):
        g = gp_ref[pl.ds(t * frame, frame), :].astype(jnp.float32)
        gt = jnp.transpose(g).astype(col_ref.dtype)
        for kt in range(3):
            part = jnp.dot(gt, col_ref[t + kt], preferred_element_type=jnp.float32)
            acc_ref[kt] = acc_ref[kt] + mask_ref[kt, t] * part
    for kt in range(3):
        flat_ref[pl.ds(kt * taps, taps), :] = jnp.transpose(acc_ref[kt])
    chips, share = mine_ref.shape[0], mine_ref.shape[1]
    first = core_ref[0] == 0
    for c in range(chips):
        even = flat_ref[pl.ds(2 * c * share, share), :]
        odd = flat_ref[pl.ds((2 * c + 1) * share, share), :]
        mine_ref[c] = jnp.where(first, even, odd)
        other_ref[c] = jnp.where(first, odd, even)


def forward_call(core, mask, early, own, ahead, cot, w, hh, ww, nout, nfr, blocks):
    frame = hh * ww
    cc = own.shape[1]
    krows = w.shape[0]
    vmem = pl.BlockSpec(memory_space=pltpu.VMEM)
    flops = 2 * 3 * frame * 9 * cc * cc * (nout + nfr)
    return pl.pallas_call(
        functools.partial(forward_kernel, hh, ww, nout, nfr),
        out_shape=(
            jax.ShapeDtypeStruct((nfr * frame, cc), jnp.bfloat16),
            jax.ShapeDtypeStruct((nout * frame, cc), jnp.bfloat16),
            jax.ShapeDtypeStruct((blocks // 2, krows // blocks, cc), jnp.float32),
            jax.ShapeDtypeStruct((blocks // 2, krows // blocks, cc), jnp.float32),
        ),
        in_specs=[pl.BlockSpec(memory_space=pltpu.SMEM), pl.BlockSpec(memory_space=pltpu.SMEM), vmem, vmem, vmem, vmem, vmem],
        out_specs=(vmem, vmem, vmem, vmem),
        scratch_shapes=[
            pltpu.VMEM((nout + 2, frame, 9 * cc), jnp.bfloat16),
            pltpu.VMEM((frame + 4 * ww, cc), jnp.float32),
            pltpu.VMEM((3, cc, 9 * cc), jnp.float32),
            pltpu.VMEM((krows, cc), jnp.float32),
        ],
        compiler_params=pltpu.CompilerParams(vmem_limit_bytes=48 * 1024 * 1024),
        cost_estimate=pl.CostEstimate(
            flops=flops,
            transcendentals=nout * frame * cc,
            bytes_accessed=2 * (early.size + own.size + ahead.size + cot.size + w.size) + 4 * krows * cc,
        ),
    )(core, mask, early, own, ahead, cot, w)


def input_grad_kernel(hh, ww, nfr, mask_ref, gp_ref, w_ref, out_ref, col_ref, pad_ref):
    frame = hh * ww
    cc = gp_ref.shape[1]
    lead = 2 * ww
    r = lax.broadcasted_iota(jnp.int32, (frame, cc), 0)
    i = r // ww
    j = r % ww
    pad_ref[...] = jnp.zeros_like(pad_ref)
    for f in range(nfr + 2):
        pad_ref[pl.ds(lead, frame), :] = gp_ref[pl.ds(f * frame, frame), :].astype(jnp.float32)
        for ky in range(3):
            for kx in range(3):
                dy, dx = 1 - ky, 1 - kx
                s = pad_ref[pl.ds(lead + dy * ww + dx, frame), :]
                valid = (i + dy >= 0) & (i + dy < hh) & (j + dx >= 0) & (j + dx < ww)
                s = jnp.where(valid, s, 0.0)
                col_ref[f, :, pl.ds((ky * 3 + kx) * cc, cc)] = s.astype(col_ref.dtype)
    taps = 9 * cc
    for t in range(nfr):
        acc = jnp.zeros((frame, cc), jnp.float32)
        for kt in range(3):
            part = jnp.dot(col_ref[t + 2 - kt], w_ref[pl.ds(kt * taps, taps), :], preferred_element_type=jnp.float32)
            acc = acc + mask_ref[kt, t] * part
        out_ref[pl.ds(t * frame, frame), :] = acc.astype(out_ref.dtype)


def input_grad_call(mask, gp, w, hh, ww, nfr):
    frame = hh * ww
    cc = gp.shape[1]
    vmem = pl.BlockSpec(memory_space=pltpu.VMEM)
    return pl.pallas_call(
        functools.partial(input_grad_kernel, hh, ww, nfr),
        out_shape=jax.ShapeDtypeStruct((nfr * frame, cc), jnp.bfloat16),
        in_specs=[pl.BlockSpec(memory_space=pltpu.SMEM), vmem, vmem],
        out_specs=vmem,
        scratch_shapes=[
            pltpu.VMEM((nfr + 2, frame, 9 * cc), jnp.bfloat16),
            pltpu.VMEM((frame + 4 * ww, cc), jnp.float32),
        ],
        compiler_params=pltpu.CompilerParams(vmem_limit_bytes=32 * 1024 * 1024),
        cost_estimate=pl.CostEstimate(
            flops=2 * 3 * frame * 9 * cc * cc * nfr, transcendentals=0, bytes_accessed=2 * (gp.size + w.size) + 2 * nfr * frame * cc
        ),
    )(mask, gp, w)


def per_device(clips, segment_ids, conv_weight, cotangent):
    nfr = clips.shape[1]
    hh = clips.shape[2]
    ww = clips.shape[3]
    cc = clips.shape[4]
    rows = nfr * hh * ww
    earlier = from_behind(clips[:, nfr - 2 :], TM, 1)[0]
    ahead = from_behind(jnp.concatenate([clips[:, :2], cotangent[:, :2]], axis=1), TM, -1)[0]
    segrow = segment_ids[0]
    segp = jnp.concatenate([jnp.full((2,), -1, jnp.int32), segrow, jnp.full((2,), -2, jnp.int32)])
    start = (lax.axis_index("chip") * lax.axis_size("core") + lax.axis_index("core")) * nfr
    seglocal = lax.dynamic_slice_in_dim(segp, start, nfr + 4, 0)
    nout = nfr + 2
    centre = seglocal[2 : 2 + nout]
    mask = jnp.stack([(seglocal[kt : kt + nout] == centre) for kt in range(3)]).astype(jnp.float32)
    tm = lax.axis_size("chip") * lax.axis_size("core")
    core = lax.axis_index("core").astype(jnp.int32).reshape(1)
    act, grad_pre, mine, other = forward_call(
        core,
        mask,
        earlier.reshape(-1, cc),
        clips.reshape(-1, cc),
        ahead.reshape(-1, cc),
        cotangent.reshape(-1, cc),
        conv_weight,
        hh,
        ww,
        nout,
        nfr,
        tm,
    )
    activated = act.reshape(clips.shape)
    count = lax.axis_size("dp") * (lax.axis_size("chip") * lax.axis_size("core")) * rows
    own = seglocal[2 : 2 + nfr]
    later_mask = jnp.stack([(seglocal[4 - kt : 4 - kt + nfr] == own) for kt in range(3)]).astype(jnp.float32)
    flipped = jnp.concatenate(
        [jnp.swapaxes(conv_weight[kt * 9 * cc : (kt + 1) * 9 * cc].reshape(9, cc, cc), 1, 2).reshape(9 * cc, cc) for kt in range(3)],
        axis=0,
    )
    grad_clips = input_grad_call(later_mask, grad_pre, flipped, hh, ww, nfr)
    total, grad_clips = reduce_weight_grad(mine, other, grad_clips)
    grad_weight = total / jnp.sqrt(jnp.float32(count))
    grad_clips = grad_clips.reshape(clips.shape)
    return (activated, grad_clips, grad_weight)


def solution(mesh):
    dp, tm = mesh.devices.shape
    cores = 2 if tm % 2 == 0 else 1
    split = Mesh(mesh.devices.reshape(dp, tm // cores, cores), ("dp", "chip", "core"))
    return jax.shard_map(
        per_device,
        mesh=split,
        in_specs=(
            P("dp", TM, None, None, None),
            P("dp", None),
            P(),
            P("dp", TM, None, None, None),
        ),
        out_specs=(P("dp", TM, None, None, None), P("dp", TM, None, None, None), P(TM, None)),
        check_vma=False,
    )
```

```python
import functools

import jax
import jax.numpy as jnp
from jax import lax
from jax.experimental import pallas as pl
from jax.experimental.pallas import tpu as pltpu
from jax.sharding import Mesh, PartitionSpec as P

TM = ("chip", "core")


def from_behind(value, axis, steps):
    count = lax.axis_size(axis)
    leading, last = (max(0, -steps), min(count, count - steps))
    return lax.ppermute(value, axis, [(source, source + steps) for source in range(leading, last)])


def reduce_weight_grad(mine, other, tie):
    dp = lax.axis_size("dp")
    cores = lax.axis_size("core")
    mine = mine + lax.ppermute(other, "core", [(i, (i + 1) % cores) for i in range(cores)])
    mine = lax.all_to_all(mine, "chip", 0, 0, tiled=True).sum(axis=0)
    mine, tie = lax.optimization_barrier((mine, tie))
    step = 1
    while step < dp:
        mine = mine + lax.ppermute(mine, "dp", [(i, i ^ step) for i in range(dp)])
        step *= 2
    return mine, tie


def im2col(frames, offset, hh, ww):
    padded = jnp.pad(frames, ((0, 0), (1, 1), (1, 1), (0, 0)))
    pieces = [
        padded[:, offset(ky) : offset(ky) + hh, offset(kx) : offset(kx) + ww]
        for ky in range(3)
        for kx in range(3)
    ]
    return jnp.concatenate(pieces, axis=3).reshape(-1, 9 * frames.shape[-1])


def forward_kernel(hh, ww, nout, nfr, core_ref, mask_ref, early_ref, own_hbm, ahead_ref, cot_hbm, w_ref, act_ref, gp_ref, mine_ref, other_ref, col_ref, pad_ref, acc_ref, flat_ref, cot_ref, cot_sem, own_ref, own_sem):
    frame = hh * ww
    cc = own_ref.shape[1]
    taps = 9 * cc
    lead = 2 * ww
    r = lax.broadcasted_iota(jnp.int32, (frame, cc), 0)
    i = r // ww
    j = r % ww
    own_copy = pltpu.make_async_copy(own_hbm, own_ref, own_sem)
    own_copy.start()
    cot_copy = pltpu.make_async_copy(cot_hbm, cot_ref, cot_sem)
    cot_copy.start()
    pad_ref[...] = jnp.zeros_like(pad_ref)
    for f in range(nout + 2):
        if f < 2:
            source = early_ref[pl.ds(f * frame, frame), :]
        elif f < nfr + 2:
            if f == 2:
                own_copy.wait()
            source = own_ref[pl.ds((f - 2) * frame, frame), :]
        else:
            source = ahead_ref[pl.ds((f - nfr - 2) * frame, frame), :]
        pad_ref[pl.ds(lead, frame), :] = source.astype(jnp.float32)
        for ky in range(3):
            for kx in range(3):
                dy, dx = ky - 1, kx - 1
                s = pad_ref[pl.ds(lead + dy * ww + dx, frame), :]
                valid = (i + dy >= 0) & (i + dy < hh) & (j + dx >= 0) & (j + dx < ww)
                s = jnp.where(valid, s, 0.0)
                col_ref[f, :, pl.ds((ky * 3 + kx) * cc, cc)] = s.astype(col_ref.dtype)
    cot_copy.wait()
    for t in range(nout):
        pre = jnp.zeros((frame, cc), jnp.float32)
        for kt in range(3):
            part = jnp.dot(col_ref[t + kt], w_ref[pl.ds(kt * taps, taps), :], preferred_element_type=jnp.float32)
            pre = pre + mask_ref[kt, t] * part
        sig = 1.0 / (1.0 + jnp.exp(-pre))
        if t < nfr:
            act_ref[pl.ds(t * frame, frame), :] = (pre * sig).astype(act_ref.dtype)
        if t < nfr:
            cot = cot_ref[pl.ds(t * frame, frame), :].astype(jnp.float32)
        else:
            cot = ahead_ref[pl.ds((t - nfr + 2) * frame, frame), :].astype(jnp.float32)
        gp_ref[pl.ds(t * frame, frame), :] = (cot * sig * (1.0 + pre * (1.0 - sig))).astype(gp_ref.dtype)
    acc_ref[...] = jnp.zeros_like(acc_ref)
    for t in range(nfr):
        g = gp_ref[pl.ds(t * frame, frame), :].astype(jnp.float32)
        gt = jnp.transpose(g).astype(col_ref.dtype)
        for kt in range(3):
            part = jnp.dot(gt, col_ref[t + kt], preferred_element_type=jnp.float32)
            acc_ref[kt] = acc_ref[kt] + mask_ref[kt, t] * part
    for kt in range(3):
        flat_ref[pl.ds(kt * taps, taps), :] = jnp.transpose(acc_ref[kt])
    chips, share = mine_ref.shape[0], mine_ref.shape[1]
    first = core_ref[0] == 0
    for c in range(chips):
        even = flat_ref[pl.ds(2 * c * share, share), :]
        odd = flat_ref[pl.ds((2 * c + 1) * share, share), :]
        mine_ref[c] = jnp.where(first, even, odd)
        other_ref[c] = jnp.where(first, odd, even)


def forward_call(core, mask, early, own, ahead, cot, w, hh, ww, nout, nfr, blocks):
    frame = hh * ww
    cc = own.shape[1]
    krows = w.shape[0]
    vmem = pl.BlockSpec(memory_space=pltpu.VMEM)
    flops = 2 * 3 * frame * 9 * cc * cc * (nout + nfr)
    return pl.pallas_call(
        functools.partial(forward_kernel, hh, ww, nout, nfr),
        out_shape=(
            jax.ShapeDtypeStruct((nfr * frame, cc), jnp.bfloat16),
            jax.ShapeDtypeStruct((nout * frame, cc), jnp.bfloat16),
            jax.ShapeDtypeStruct((blocks // 2, krows // blocks, cc), jnp.float32),
            jax.ShapeDtypeStruct((blocks // 2, krows // blocks, cc), jnp.float32),
        ),
        in_specs=[pl.BlockSpec(memory_space=pltpu.SMEM), pl.BlockSpec(memory_space=pltpu.SMEM), vmem, pl.BlockSpec(memory_space=pltpu.HBM), vmem, pl.BlockSpec(memory_space=pltpu.HBM), vmem],
        out_specs=(vmem, vmem, vmem, vmem),
        scratch_shapes=[
            pltpu.VMEM((nout + 2, frame, 9 * cc), jnp.bfloat16),
            pltpu.VMEM((frame + 4 * ww, cc), jnp.float32),
            pltpu.VMEM((3, cc, 9 * cc), jnp.float32),
            pltpu.VMEM((krows, cc), jnp.float32),
            pltpu.VMEM(cot.shape, cot.dtype),
            pltpu.SemaphoreType.DMA,
            pltpu.VMEM(own.shape, own.dtype),
            pltpu.SemaphoreType.DMA,
        ],
        compiler_params=pltpu.CompilerParams(vmem_limit_bytes=48 * 1024 * 1024),
        cost_estimate=pl.CostEstimate(
            flops=flops,
            transcendentals=nout * frame * cc,
            bytes_accessed=2 * (early.size + own.size + ahead.size + cot.size + w.size) + 4 * krows * cc,
        ),
    )(core, mask, early, own, ahead, cot, w)


def input_grad_kernel(hh, ww, nfr, mask_ref, gp_ref, w_ref, out_ref, col_ref, pad_ref):
    frame = hh * ww
    cc = gp_ref.shape[1]
    lead = 2 * ww
    r = lax.broadcasted_iota(jnp.int32, (frame, cc), 0)
    i = r // ww
    j = r % ww
    pad_ref[...] = jnp.zeros_like(pad_ref)
    for f in range(nfr + 2):
        pad_ref[pl.ds(lead, frame), :] = gp_ref[pl.ds(f * frame, frame), :].astype(jnp.float32)
        for ky in range(3):
            for kx in range(3):
                dy, dx = 1 - ky, 1 - kx
                s = pad_ref[pl.ds(lead + dy * ww + dx, frame), :]
                valid = (i + dy >= 0) & (i + dy < hh) & (j + dx >= 0) & (j + dx < ww)
                s = jnp.where(valid, s, 0.0)
                col_ref[f, :, pl.ds((ky * 3 + kx) * cc, cc)] = s.astype(col_ref.dtype)
    taps = 9 * cc
    for t in range(nfr):
        acc = jnp.zeros((frame, cc), jnp.float32)
        for kt in range(3):
            part = jnp.dot(col_ref[t + 2 - kt], w_ref[pl.ds(kt * taps, taps), :], preferred_element_type=jnp.float32)
            acc = acc + mask_ref[kt, t] * part
        out_ref[pl.ds(t * frame, frame), :] = acc.astype(out_ref.dtype)


def input_grad_call(mask, gp, w, hh, ww, nfr):
    frame = hh * ww
    cc = gp.shape[1]
    vmem = pl.BlockSpec(memory_space=pltpu.VMEM)
    return pl.pallas_call(
        functools.partial(input_grad_kernel, hh, ww, nfr),
        out_shape=jax.ShapeDtypeStruct((nfr * frame, cc), jnp.bfloat16),
        in_specs=[pl.BlockSpec(memory_space=pltpu.SMEM), vmem, vmem],
        out_specs=vmem,
        scratch_shapes=[
            pltpu.VMEM((nfr + 2, frame, 9 * cc), jnp.bfloat16),
            pltpu.VMEM((frame + 4 * ww, cc), jnp.float32),
        ],
        compiler_params=pltpu.CompilerParams(vmem_limit_bytes=32 * 1024 * 1024),
        cost_estimate=pl.CostEstimate(
            flops=2 * 3 * frame * 9 * cc * cc * nfr, transcendentals=0, bytes_accessed=2 * (gp.size + w.size) + 2 * nfr * frame * cc
        ),
    )(mask, gp, w)


def per_device(clips, segment_ids, conv_weight, cotangent):
    nfr = clips.shape[1]
    hh = clips.shape[2]
    ww = clips.shape[3]
    cc = clips.shape[4]
    rows = nfr * hh * ww
    earlier = from_behind(clips[:, nfr - 2 :], TM, 1)[0]
    ahead = from_behind(jnp.concatenate([clips[:, :2], cotangent[:, :2]], axis=1), TM, -1)[0]
    segrow = segment_ids[0]
    segp = jnp.concatenate([jnp.full((2,), -1, jnp.int32), segrow, jnp.full((2,), -2, jnp.int32)])
    start = (lax.axis_index("chip") * lax.axis_size("core") + lax.axis_index("core")) * nfr
    seglocal = lax.dynamic_slice_in_dim(segp, start, nfr + 4, 0)
    nout = nfr + 2
    centre = seglocal[2 : 2 + nout]
    mask = jnp.stack([(seglocal[kt : kt + nout] == centre) for kt in range(3)]).astype(jnp.float32)
    tm = lax.axis_size("chip") * lax.axis_size("core")
    core = lax.axis_index("core").astype(jnp.int32).reshape(1)
    act, grad_pre, mine, other = forward_call(
        core,
        mask,
        earlier.reshape(-1, cc),
        clips.reshape(-1, cc),
        ahead.reshape(-1, cc),
        cotangent.reshape(-1, cc),
        conv_weight,
        hh,
        ww,
        nout,
        nfr,
        tm,
    )
    activated = act.reshape(clips.shape)
    count = lax.axis_size("dp") * (lax.axis_size("chip") * lax.axis_size("core")) * rows
    own = seglocal[2 : 2 + nfr]
    later_mask = jnp.stack([(seglocal[4 - kt : 4 - kt + nfr] == own) for kt in range(3)]).astype(jnp.float32)
    flipped = jnp.concatenate(
        [jnp.swapaxes(conv_weight[kt * 9 * cc : (kt + 1) * 9 * cc].reshape(9, cc, cc), 1, 2).reshape(9 * cc, cc) for kt in range(3)],
        axis=0,
    )
    grad_clips = input_grad_call(later_mask, grad_pre, flipped, hh, ww, nfr)
    total, grad_clips = reduce_weight_grad(mine, other, grad_clips)
    grad_weight = total / jnp.sqrt(jnp.float32(count))
    grad_clips = grad_clips.reshape(clips.shape)
    return (activated, grad_clips, grad_weight)


def solution(mesh):
    dp, tm = mesh.devices.shape
    cores = 2 if tm % 2 == 0 else 1
    split = Mesh(mesh.devices.reshape(dp, tm // cores, cores), ("dp", "chip", "core"))
    return jax.shard_map(
        per_device,
        mesh=split,
        in_specs=(
            P("dp", TM, None, None, None),
            P("dp", None),
            P(),
            P("dp", TM, None, None, None),
        ),
        out_specs=(P("dp", TM, None, None, None), P("dp", TM, None, None, None), P(TM, None)),
        check_vma=False,
    )
```

```python
import functools

import jax
import jax.numpy as jnp
from jax import lax
from jax.experimental import pallas as pl
from jax.experimental.pallas import tpu as pltpu
from jax.sharding import Mesh, PartitionSpec as P

TM = ("chip", "core")


def from_behind(value, axis, steps):
    count = lax.axis_size(axis)
    leading, last = (max(0, -steps), min(count, count - steps))
    return lax.ppermute(value, axis, [(source, source + steps) for source in range(leading, last)])


def reduce_weight_grad(mine, other, tie):
    dp = lax.axis_size("dp")
    cores = lax.axis_size("core")
    mine = mine + lax.ppermute(other, "core", [(i, (i + 1) % cores) for i in range(cores)])
    chips = lax.axis_size("chip")
    mine = lax.all_to_all(mine, "chip", 0, 0, tiled=True)
    mine = mine.reshape(chips, mine.shape[0] // chips, mine.shape[1]).sum(axis=0)
    mine, tie = lax.optimization_barrier((mine, tie))
    step = 1
    while step < dp:
        mine = mine + lax.ppermute(mine, "dp", [(i, i ^ step) for i in range(dp)])
        step *= 2
    return mine, tie


def im2col(frames, offset, hh, ww):
    padded = jnp.pad(frames, ((0, 0), (1, 1), (1, 1), (0, 0)))
    pieces = [
        padded[:, offset(ky) : offset(ky) + hh, offset(kx) : offset(kx) + ww]
        for ky in range(3)
        for kx in range(3)
    ]
    return jnp.concatenate(pieces, axis=3).reshape(-1, 9 * frames.shape[-1])


def forward_kernel(hh, ww, nout, nfr, blocks_of, core_ref, mask_ref, early_ref, own_ref, ahead_ref, cot_ref, w_ref, act_ref, gp_ref, mine_ref, other_ref, col_ref, pad_ref, acc_ref, flat_ref):
    frame = hh * ww
    cc = own_ref.shape[1]
    taps = 9 * cc
    lead = 2 * ww
    r = lax.broadcasted_iota(jnp.int32, (frame, cc), 0)
    i = r // ww
    j = r % ww
    pad_ref[...] = jnp.zeros_like(pad_ref)
    for f in range(nout + 2):
        if f < 2:
            source = early_ref[pl.ds(f * frame, frame), :]
        elif f < nfr + 2:
            source = own_ref[pl.ds((f - 2) * frame, frame), :]
        else:
            source = ahead_ref[pl.ds((f - nfr - 2) * frame, frame), :]
        pad_ref[pl.ds(lead, frame), :] = source.astype(jnp.float32)
        for ky in range(3):
            for kx in range(3):
                dy, dx = ky - 1, kx - 1
                s = pad_ref[pl.ds(lead + dy * ww + dx, frame), :]
                valid = (i + dy >= 0) & (i + dy < hh) & (j + dx >= 0) & (j + dx < ww)
                s = jnp.where(valid, s, 0.0)
                col_ref[f, :, pl.ds((ky * 3 + kx) * cc, cc)] = s.astype(col_ref.dtype)
    for t in range(nout):
        pre = jnp.zeros((frame, cc), jnp.float32)
        for kt in range(3):
            part = jnp.dot(col_ref[t + kt], w_ref[pl.ds(kt * taps, taps), :], preferred_element_type=jnp.float32)
            pre = pre + mask_ref[kt, t] * part
        sig = 1.0 / (1.0 + jnp.exp(-pre))
        if t < nfr:
            act_ref[pl.ds(t * frame, frame), :] = (pre * sig).astype(act_ref.dtype)
        if t < nfr:
            cot = cot_ref[pl.ds(t * frame, frame), :].astype(jnp.float32)
        else:
            cot = ahead_ref[pl.ds((t - nfr + 2) * frame, frame), :].astype(jnp.float32)
        gp_ref[pl.ds(t * frame, frame), :] = (cot * sig * (1.0 + pre * (1.0 - sig))).astype(gp_ref.dtype)
    acc_ref[...] = jnp.zeros_like(acc_ref)
    for t in range(nfr):
        g = gp_ref[pl.ds(t * frame, frame), :].astype(jnp.float32)
        gt = jnp.transpose(g).astype(col_ref.dtype)
        for kt in range(3):
            part = jnp.dot(gt, col_ref[t + kt], preferred_element_type=jnp.float32)
            acc_ref[kt] = acc_ref[kt] + mask_ref[kt, t] * part
    for kt in range(3):
        flat_ref[pl.ds(kt * taps, taps), :] = jnp.transpose(acc_ref[kt])
    chips, share = blocks_of, mine_ref.shape[0] // blocks_of
    first = core_ref[0] == 0
    for c in range(chips):
        even = flat_ref[pl.ds(2 * c * share, share), :]
        odd = flat_ref[pl.ds((2 * c + 1) * share, share), :]
        mine_ref[pl.ds(c * share, share), :] = jnp.where(first, even, odd)
        other_ref[pl.ds(c * share, share), :] = jnp.where(first, odd, even)


def forward_call(core, mask, early, own, ahead, cot, w, hh, ww, nout, nfr, blocks):
    frame = hh * ww
    cc = own.shape[1]
    krows = w.shape[0]
    vmem = pl.BlockSpec(memory_space=pltpu.VMEM)
    flops = 2 * 3 * frame * 9 * cc * cc * (nout + nfr)
    return pl.pallas_call(
        functools.partial(forward_kernel, hh, ww, nout, nfr, blocks // 2),
        out_shape=(
            jax.ShapeDtypeStruct((nfr * frame, cc), jnp.bfloat16),
            jax.ShapeDtypeStruct((nout * frame, cc), jnp.bfloat16),
            jax.ShapeDtypeStruct((krows // 2, cc), jnp.float32),
            jax.ShapeDtypeStruct((krows // 2, cc), jnp.float32),
        ),
        in_specs=[pl.BlockSpec(memory_space=pltpu.SMEM), pl.BlockSpec(memory_space=pltpu.SMEM), vmem, vmem, vmem, vmem, vmem],
        out_specs=(vmem, vmem, vmem, vmem),
        scratch_shapes=[
            pltpu.VMEM((nout + 2, frame, 9 * cc), jnp.bfloat16),
            pltpu.VMEM((frame + 4 * ww, cc), jnp.float32),
            pltpu.VMEM((3, cc, 9 * cc), jnp.float32),
            pltpu.VMEM((krows, cc), jnp.float32),
        ],
        compiler_params=pltpu.CompilerParams(vmem_limit_bytes=48 * 1024 * 1024),
        cost_estimate=pl.CostEstimate(
            flops=flops,
            transcendentals=nout * frame * cc,
            bytes_accessed=2 * (early.size + own.size + ahead.size + cot.size + w.size) + 4 * krows * cc,
        ),
    )(core, mask, early, own, ahead, cot, w)


def input_grad_kernel(hh, ww, nfr, mask_ref, gp_ref, w_ref, out_ref, col_ref, pad_ref):
    frame = hh * ww
    cc = gp_ref.shape[1]
    lead = 2 * ww
    r = lax.broadcasted_iota(jnp.int32, (frame, cc), 0)
    i = r // ww
    j = r % ww
    pad_ref[...] = jnp.zeros_like(pad_ref)
    for f in range(nfr + 2):
        pad_ref[pl.ds(lead, frame), :] = gp_ref[pl.ds(f * frame, frame), :].astype(jnp.float32)
        for ky in range(3):
            for kx in range(3):
                dy, dx = 1 - ky, 1 - kx
                s = pad_ref[pl.ds(lead + dy * ww + dx, frame), :]
                valid = (i + dy >= 0) & (i + dy < hh) & (j + dx >= 0) & (j + dx < ww)
                s = jnp.where(valid, s, 0.0)
                col_ref[f, :, pl.ds((ky * 3 + kx) * cc, cc)] = s.astype(col_ref.dtype)
    taps = 9 * cc
    for t in range(nfr):
        acc = jnp.zeros((frame, cc), jnp.float32)
        for kt in range(3):
            part = jnp.dot(col_ref[t + 2 - kt], w_ref[pl.ds(kt * taps, taps), :], preferred_element_type=jnp.float32)
            acc = acc + mask_ref[kt, t] * part
        out_ref[pl.ds(t * frame, frame), :] = acc.astype(out_ref.dtype)


def input_grad_call(mask, gp, w, hh, ww, nfr):
    frame = hh * ww
    cc = gp.shape[1]
    vmem = pl.BlockSpec(memory_space=pltpu.VMEM)
    return pl.pallas_call(
        functools.partial(input_grad_kernel, hh, ww, nfr),
        out_shape=jax.ShapeDtypeStruct((nfr * frame, cc), jnp.bfloat16),
        in_specs=[pl.BlockSpec(memory_space=pltpu.SMEM), vmem, vmem],
        out_specs=vmem,
        scratch_shapes=[
            pltpu.VMEM((nfr + 2, frame, 9 * cc), jnp.bfloat16),
            pltpu.VMEM((frame + 4 * ww, cc), jnp.float32),
        ],
        compiler_params=pltpu.CompilerParams(vmem_limit_bytes=32 * 1024 * 1024),
        cost_estimate=pl.CostEstimate(
            flops=2 * 3 * frame * 9 * cc * cc * nfr, transcendentals=0, bytes_accessed=2 * (gp.size + w.size) + 2 * nfr * frame * cc
        ),
    )(mask, gp, w)


def per_device(clips, segment_ids, conv_weight, cotangent):
    nfr = clips.shape[1]
    hh = clips.shape[2]
    ww = clips.shape[3]
    cc = clips.shape[4]
    rows = nfr * hh * ww
    earlier = from_behind(clips[:, nfr - 2 :], TM, 1)[0]
    ahead = from_behind(jnp.concatenate([clips[:, :2], cotangent[:, :2]], axis=1), TM, -1)[0]
    segrow = segment_ids[0]
    segp = jnp.concatenate([jnp.full((2,), -1, jnp.int32), segrow, jnp.full((2,), -2, jnp.int32)])
    start = (lax.axis_index("chip") * lax.axis_size("core") + lax.axis_index("core")) * nfr
    seglocal = lax.dynamic_slice_in_dim(segp, start, nfr + 4, 0)
    nout = nfr + 2
    centre = seglocal[2 : 2 + nout]
    mask = jnp.stack([(seglocal[kt : kt + nout] == centre) for kt in range(3)]).astype(jnp.float32)
    tm = lax.axis_size("chip") * lax.axis_size("core")
    core = lax.axis_index("core").astype(jnp.int32).reshape(1)
    act, grad_pre, mine, other = forward_call(
        core,
        mask,
        earlier.reshape(-1, cc),
        clips.reshape(-1, cc),
        ahead.reshape(-1, cc),
        cotangent.reshape(-1, cc),
        conv_weight,
        hh,
        ww,
        nout,
        nfr,
        tm,
    )
    activated = act.reshape(clips.shape)
    count = lax.axis_size("dp") * (lax.axis_size("chip") * lax.axis_size("core")) * rows
    own = seglocal[2 : 2 + nfr]
    later_mask = jnp.stack([(seglocal[4 - kt : 4 - kt + nfr] == own) for kt in range(3)]).astype(jnp.float32)
    flipped = jnp.concatenate(
        [jnp.swapaxes(conv_weight[kt * 9 * cc : (kt + 1) * 9 * cc].reshape(9, cc, cc), 1, 2).reshape(9 * cc, cc) for kt in range(3)],
        axis=0,
    )
    grad_clips = input_grad_call(later_mask, grad_pre, flipped, hh, ww, nfr)
    total, grad_clips = reduce_weight_grad(mine, other, grad_clips)
    grad_weight = total / jnp.sqrt(jnp.float32(count))
    grad_clips = grad_clips.reshape(clips.shape)
    return (activated, grad_clips, grad_weight)


def solution(mesh):
    dp, tm = mesh.devices.shape
    cores = 2 if tm % 2 == 0 else 1
    split = Mesh(mesh.devices.reshape(dp, tm // cores, cores), ("dp", "chip", "core"))
    return jax.shard_map(
        per_device,
        mesh=split,
        in_specs=(
            P("dp", TM, None, None, None),
            P("dp", None),
            P(),
            P("dp", TM, None, None, None),
        ),
        out_specs=(P("dp", TM, None, None, None), P("dp", TM, None, None, None), P(TM, None)),
        check_vma=False,
    )
```

```python
import functools

import jax
import jax.numpy as jnp
from jax import lax
from jax.experimental import pallas as pl
from jax.experimental.pallas import tpu as pltpu
from jax.sharding import Mesh, PartitionSpec as P

TM = ("chip", "core")


def from_behind(value, axis, steps):
    count = lax.axis_size(axis)
    leading, last = (max(0, -steps), min(count, count - steps))
    return lax.ppermute(value, axis, [(source, source + steps) for source in range(leading, last)])


def reduce_weight_grad(mine, other, tie, share):
    dp = lax.axis_size("dp")
    cores = lax.axis_size("core")
    mine = mine + lax.ppermute(other, "core", [(i, (i + 1) % cores) for i in range(cores)])
    chips = lax.axis_size("chip")
    mine = lax.all_to_all(mine, "chip", 0, 0, tiled=True)
    mine = mine.reshape(chips, mine.shape[0] // chips, mine.shape[1]).sum(axis=0)[:share]
    mine, tie = lax.optimization_barrier((mine, tie))
    step = 1
    while step < dp:
        mine = mine + lax.ppermute(mine, "dp", [(i, i ^ step) for i in range(dp)])
        step *= 2
    return mine, tie


def im2col(frames, offset, hh, ww):
    padded = jnp.pad(frames, ((0, 0), (1, 1), (1, 1), (0, 0)))
    pieces = [
        padded[:, offset(ky) : offset(ky) + hh, offset(kx) : offset(kx) + ww]
        for ky in range(3)
        for kx in range(3)
    ]
    return jnp.concatenate(pieces, axis=3).reshape(-1, 9 * frames.shape[-1])


def forward_kernel(hh, ww, nout, nfr, blocks_of, core_ref, mask_ref, early_ref, own_ref, ahead_ref, cot_ref, w_ref, act_ref, gp_ref, mine_ref, other_ref, col_ref, pad_ref, acc_ref, flat_ref):
    frame = hh * ww
    cc = own_ref.shape[1]
    taps = 9 * cc
    lead = 2 * ww
    r = lax.broadcasted_iota(jnp.int32, (frame, cc), 0)
    i = r // ww
    j = r % ww
    pad_ref[...] = jnp.zeros_like(pad_ref)
    for f in range(nout + 2):
        if f < 2:
            source = early_ref[pl.ds(f * frame, frame), :]
        elif f < nfr + 2:
            source = own_ref[pl.ds((f - 2) * frame, frame), :]
        else:
            source = ahead_ref[pl.ds((f - nfr - 2) * frame, frame), :]
        pad_ref[pl.ds(lead, frame), :] = source.astype(jnp.float32)
        for ky in range(3):
            for kx in range(3):
                dy, dx = ky - 1, kx - 1
                s = pad_ref[pl.ds(lead + dy * ww + dx, frame), :]
                valid = (i + dy >= 0) & (i + dy < hh) & (j + dx >= 0) & (j + dx < ww)
                s = jnp.where(valid, s, 0.0)
                col_ref[f, :, pl.ds((ky * 3 + kx) * cc, cc)] = s.astype(col_ref.dtype)
    for t in range(nout):
        pre = jnp.zeros((frame, cc), jnp.float32)
        for kt in range(3):
            part = jnp.dot(col_ref[t + kt], w_ref[pl.ds(kt * taps, taps), :], preferred_element_type=jnp.float32)
            pre = pre + mask_ref[kt, t] * part
        sig = 1.0 / (1.0 + jnp.exp(-pre))
        if t < nfr:
            act_ref[pl.ds(t * frame, frame), :] = (pre * sig).astype(act_ref.dtype)
        if t < nfr:
            cot = cot_ref[pl.ds(t * frame, frame), :].astype(jnp.float32)
        else:
            cot = ahead_ref[pl.ds((t - nfr + 2) * frame, frame), :].astype(jnp.float32)
        gp_ref[pl.ds(t * frame, frame), :] = (cot * sig * (1.0 + pre * (1.0 - sig))).astype(gp_ref.dtype)
    acc_ref[...] = jnp.zeros_like(acc_ref)
    for t in range(nfr):
        g = gp_ref[pl.ds(t * frame, frame), :].astype(jnp.float32)
        gt = jnp.transpose(g).astype(col_ref.dtype)
        for kt in range(3):
            part = jnp.dot(gt, col_ref[t + kt], preferred_element_type=jnp.float32)
            acc_ref[kt] = acc_ref[kt] + mask_ref[kt, t] * part
    for kt in range(3):
        flat_ref[pl.ds(kt * taps, taps), :] = jnp.transpose(acc_ref[kt])
    chips, slot = blocks_of, mine_ref.shape[0] // blocks_of
    share = flat_ref.shape[0] // (2 * chips)
    first = core_ref[0] == 0
    fill = jnp.zeros((slot - share, cc), jnp.float32)
    for c in range(chips):
        even = jnp.concatenate([flat_ref[pl.ds(2 * c * share, share), :], fill], axis=0)
        odd = jnp.concatenate([flat_ref[pl.ds((2 * c + 1) * share, share), :], fill], axis=0)
        mine_ref[pl.ds(c * slot, slot), :] = jnp.where(first, even, odd)
        other_ref[pl.ds(c * slot, slot), :] = jnp.where(first, odd, even)


def forward_call(core, mask, early, own, ahead, cot, w, hh, ww, nout, nfr, blocks):
    frame = hh * ww
    cc = own.shape[1]
    krows = w.shape[0]
    slot = -(-(krows // blocks) // 8) * 8
    vmem = pl.BlockSpec(memory_space=pltpu.VMEM)
    flops = 2 * 3 * frame * 9 * cc * cc * (nout + nfr)
    return pl.pallas_call(
        functools.partial(forward_kernel, hh, ww, nout, nfr, blocks // 2),
        out_shape=(
            jax.ShapeDtypeStruct((nfr * frame, cc), jnp.bfloat16),
            jax.ShapeDtypeStruct((nout * frame, cc), jnp.bfloat16),
            jax.ShapeDtypeStruct((blocks // 2 * slot, cc), jnp.float32),
            jax.ShapeDtypeStruct((blocks // 2 * slot, cc), jnp.float32),
        ),
        in_specs=[pl.BlockSpec(memory_space=pltpu.SMEM), pl.BlockSpec(memory_space=pltpu.SMEM), vmem, vmem, vmem, vmem, vmem],
        out_specs=(vmem, vmem, vmem, vmem),
        scratch_shapes=[
            pltpu.VMEM((nout + 2, frame, 9 * cc), jnp.bfloat16),
            pltpu.VMEM((frame + 4 * ww, cc), jnp.float32),
            pltpu.VMEM((3, cc, 9 * cc), jnp.float32),
            pltpu.VMEM((krows, cc), jnp.float32),
        ],
        compiler_params=pltpu.CompilerParams(vmem_limit_bytes=48 * 1024 * 1024),
        cost_estimate=pl.CostEstimate(
            flops=flops,
            transcendentals=nout * frame * cc,
            bytes_accessed=2 * (early.size + own.size + ahead.size + cot.size + w.size) + 4 * krows * cc,
        ),
    )(core, mask, early, own, ahead, cot, w)


def input_grad_kernel(hh, ww, nfr, mask_ref, gp_ref, w_ref, out_ref, col_ref, pad_ref):
    frame = hh * ww
    cc = gp_ref.shape[1]
    lead = 2 * ww
    r = lax.broadcasted_iota(jnp.int32, (frame, cc), 0)
    i = r // ww
    j = r % ww
    pad_ref[...] = jnp.zeros_like(pad_ref)
    for f in range(nfr + 2):
        pad_ref[pl.ds(lead, frame), :] = gp_ref[pl.ds(f * frame, frame), :].astype(jnp.float32)
        for ky in range(3):
            for kx in range(3):
                dy, dx = 1 - ky, 1 - kx
                s = pad_ref[pl.ds(lead + dy * ww + dx, frame), :]
                valid = (i + dy >= 0) & (i + dy < hh) & (j + dx >= 0) & (j + dx < ww)
                s = jnp.where(valid, s, 0.0)
                col_ref[f, :, pl.ds((ky * 3 + kx) * cc, cc)] = s.astype(col_ref.dtype)
    taps = 9 * cc
    for t in range(nfr):
        acc = jnp.zeros((frame, cc), jnp.float32)
        for kt in range(3):
            part = jnp.dot(col_ref[t + 2 - kt], w_ref[pl.ds(kt * taps, taps), :], preferred_element_type=jnp.float32)
            acc = acc + mask_ref[kt, t] * part
        out_ref[pl.ds(t * frame, frame), :] = acc.astype(out_ref.dtype)


def input_grad_call(mask, gp, w, hh, ww, nfr):
    frame = hh * ww
    cc = gp.shape[1]
    vmem = pl.BlockSpec(memory_space=pltpu.VMEM)
    return pl.pallas_call(
        functools.partial(input_grad_kernel, hh, ww, nfr),
        out_shape=jax.ShapeDtypeStruct((nfr * frame, cc), jnp.bfloat16),
        in_specs=[pl.BlockSpec(memory_space=pltpu.SMEM), vmem, vmem],
        out_specs=vmem,
        scratch_shapes=[
            pltpu.VMEM((nfr + 2, frame, 9 * cc), jnp.bfloat16),
            pltpu.VMEM((frame + 4 * ww, cc), jnp.float32),
        ],
        compiler_params=pltpu.CompilerParams(vmem_limit_bytes=32 * 1024 * 1024),
        cost_estimate=pl.CostEstimate(
            flops=2 * 3 * frame * 9 * cc * cc * nfr, transcendentals=0, bytes_accessed=2 * (gp.size + w.size) + 2 * nfr * frame * cc
        ),
    )(mask, gp, w)


def per_device(clips, segment_ids, conv_weight, cotangent):
    nfr = clips.shape[1]
    hh = clips.shape[2]
    ww = clips.shape[3]
    cc = clips.shape[4]
    rows = nfr * hh * ww
    earlier = from_behind(clips[:, nfr - 2 :], TM, 1)[0]
    ahead = from_behind(jnp.concatenate([clips[:, :2], cotangent[:, :2]], axis=1), TM, -1)[0]
    segrow = segment_ids[0]
    segp = jnp.concatenate([jnp.full((2,), -1, jnp.int32), segrow, jnp.full((2,), -2, jnp.int32)])
    start = (lax.axis_index("chip") * lax.axis_size("core") + lax.axis_index("core")) * nfr
    seglocal = lax.dynamic_slice_in_dim(segp, start, nfr + 4, 0)
    nout = nfr + 2
    centre = seglocal[2 : 2 + nout]
    mask = jnp.stack([(seglocal[kt : kt + nout] == centre) for kt in range(3)]).astype(jnp.float32)
    tm = lax.axis_size("chip") * lax.axis_size("core")
    core = lax.axis_index("core").astype(jnp.int32).reshape(1)
    act, grad_pre, mine, other = forward_call(
        core,
        mask,
        earlier.reshape(-1, cc),
        clips.reshape(-1, cc),
        ahead.reshape(-1, cc),
        cotangent.reshape(-1, cc),
        conv_weight,
        hh,
        ww,
        nout,
        nfr,
        tm,
    )
    activated = act.reshape(clips.shape)
    count = lax.axis_size("dp") * (lax.axis_size("chip") * lax.axis_size("core")) * rows
    own = seglocal[2 : 2 + nfr]
    later_mask = jnp.stack([(seglocal[4 - kt : 4 - kt + nfr] == own) for kt in range(3)]).astype(jnp.float32)
    flipped = jnp.concatenate(
        [jnp.swapaxes(conv_weight[kt * 9 * cc : (kt + 1) * 9 * cc].reshape(9, cc, cc), 1, 2).reshape(9 * cc, cc) for kt in range(3)],
        axis=0,
    )
    grad_clips = input_grad_call(later_mask, grad_pre, flipped, hh, ww, nfr)
    total, grad_clips = reduce_weight_grad(mine, other, grad_clips, conv_weight.shape[0] // tm)
    grad_weight = total / jnp.sqrt(jnp.float32(count))
    grad_clips = grad_clips.reshape(clips.shape)
    return (activated, grad_clips, grad_weight)


def solution(mesh):
    dp, tm = mesh.devices.shape
    cores = 2 if tm % 2 == 0 else 1
    split = Mesh(mesh.devices.reshape(dp, tm // cores, cores), ("dp", "chip", "core"))
    return jax.shard_map(
        per_device,
        mesh=split,
        in_specs=(
            P("dp", TM, None, None, None),
            P("dp", None),
            P(),
            P("dp", TM, None, None, None),
        ),
        out_specs=(P("dp", TM, None, None, None), P("dp", TM, None, None, None), P(TM, None)),
        check_vma=False,
    )
```
